256 devices in a mesh: space: 16 (over z_lo, y), view: 16 (over x, z_hi, core).
Axes of the slice: x: 4, y: 4, z: 8 (z_hi: 2, z_lo: 4; z = z_hi * 4 + z_lo), core: 2. Of those that a mesh axis runs over, the one named last changes fastest.
Arguments:
- estimate: float32 [16, 64, 4096], P('space', None, 'view'), may hold values from 0.5 to 2
- measured: float32 [16, 16, 64, 4096], P('view', 'space'), may hold values from 0.2 to 5
- kernel_x: float32 [16, 7], P('view'), may hold values from 0.2 to 1
- kernel_y: float32 [16, 7], P('view'), may hold values from 0.2 to 1
- kernel_z: float32 [16, 15], P('view'), may hold values from 0.2 to 1
- neighbors: int32 [16, 6], P('space'), may hold values from -1 to 15, as said below
- inside: int32 [16], P('space'), may hold values 0 or 1
Outputs:
- deconvolved: float32 [16, 64, 4096], P('space', None, 'view')
The draws below stay inside these ranges and needn't reach their ends.
Inputs may be any that keep to these rules, and one draw needn't show every extreme that they name: neighbors[b, f] is the brick across face f of brick b (faces in order: low and high along the first, second and third cell dimension), or -1 at the window's border; if neighbors[b, f] = c then neighbors[c, f + 1 - 2 (f % 2)] = b; the window is a box of 2 x 2 x (4) bricks, and the 1 bricks of one index of space lie in a row along the third dimension.
All inputs are finite; a program needn't handle non-finite values. No bound on the sum of `inside` on one device may be relied on, other than what follows from the above.
Results may differ from the reference program's by a relative error of at most 0.0001.
Values sent between devices are 32-bit elements; how exact they have to be, the bound alone decides.
No kernel may reach another device: no remote copies, remote signals or barrier semaphores. Data moves between devices by JAX's collectives and lax.ppermute only.
A program may use at most 128 MiB of HBM per device.

```python
import math
import jax
import jax.numpy as jnp
import numpy as np
from jax import lax

S = 64
BR_DEV = 1
ITERS = 2
TAPS_XY = 7
TAPS_Z = 15
VIEWS = 16
BRICKS = 16


def base_layout(unit_count):
    half_units = unit_count // 2
    core_cells = [(0, 0, 0), (0, 0, 1), (1, 1, 0), (0, 1, 0), (1, 0, 0), (0, 1, 1), (1, 1, 1), (1, 0, 1)]
    base_table = [None] * unit_count
    for core_index in range(8):
        target = core_index if core_index < 4 else half_units + core_index - 4
        base_table[target] = core_cells[core_index]
    square_order = [(0, 0), (0, 1), (1, 1), (1, 0)]
    placed = 0
    for target in range(unit_count):
        if base_table[target] is None:
            layer_no = 2 + placed // 4
            corner = placed % 4 if layer_no % 2 == 0 else 3 - placed % 4
            base_table[target] = (square_order[corner][0], square_order[corner][1], layer_no)
            placed = placed + 1
    return np.array(base_table, dtype=np.int32)


def draw_neighbors(key, part):
    unit_count = BRICKS // BR_DEV
    base_table = jnp.asarray(base_layout(unit_count))
    offset = jax.random.randint(key, (), 0, unit_count, dtype=jnp.int32)
    mirror_bits = jax.random.randint(jax.random.fold_in(key, 1), (3,), 0, 2, dtype=jnp.int32)
    brick_ids = jnp.arange(BRICKS, dtype=jnp.int32)
    unit_ids = brick_ids // BR_DEV
    row_place = brick_ids % BR_DEV
    base_ids = (unit_ids - offset) % unit_count
    unit_cells = base_table[base_ids]
    box_depth = unit_count // 4 * BR_DEV
    cell_x = unit_cells[:, 0]
    cell_y = unit_cells[:, 1]
    cell_z = unit_cells[:, 2] * BR_DEV + row_place
    cell_x = jnp.where(mirror_bits[0] == 1, 1 - cell_x, cell_x)
    cell_y = jnp.where(mirror_bits[1] == 1, 1 - cell_y, cell_y)
    cell_z = jnp.where(mirror_bits[2] == 1, box_depth - 1 - cell_z, cell_z)

    def locate(delta_x, delta_y, delta_z):
        matches = (cell_x[None, :] == cell_x[:, None] + delta_x) & (cell_y[None, :] == cell_y[:, None] + delta_y) & (cell_z[None, :] == cell_z[:, None] + delta_z)
        present = jnp.any(matches, axis=1)
        position = jnp.sum(matches.astype(jnp.int32) * brick_ids[None, :], axis=1)
        return jnp.where(present, position, -1)
    stacked = jnp.stack([locate(-1, 0, 0), locate(1, 0, 0), locate(0, -1, 0), locate(0, 1, 0), locate(0, 0, -1), locate(0, 0, 1)], axis=1)
    return stacked.astype(jnp.int32)


def plant(entries, key, smallest, largest):
    extent = entries.shape
    spot = [jax.random.randint(jax.random.fold_in(key, axis), (), 0, extent[axis]) for axis in range(len(extent))]
    entries = entries.at[tuple(spot)].set(smallest)
    longest = extent.index(max(extent))
    spot[longest] = (spot[longest] + 1) % extent[longest]
    return entries.at[tuple(spot)].set(largest)


def block_levels(own_key, shape, shards, low, largest):
    loudness, own = 1.0, jax.random.fold_in(own_key, 6)
    for dim, shards_of in shards:
        draws = jnp.exp(jax.random.uniform(jax.random.fold_in(own, dim), (shards_of,), jnp.float32, low / len(shards), largest / len(shards)))
        loudness = loudness * jnp.repeat(draws, shape[dim] // shards_of).reshape([-1 if axis == dim else 1 for axis in range(len(shape))])
    return loudness


def setup_inputs(seed: int = 0) -> dict:
    keys = jax.random.split(jax.random.key(seed), 8)
    estimate = jnp.clip(jnp.exp(math.log(2.0) - 1.3862944 * jax.random.uniform(keys[0], (BRICKS, S, S * S), jnp.float32) ** block_levels(keys[0], (BRICKS, S, S * S), ((0, 16), (2, 16)), -0.2, 0.2)), 0.5, 2.0)
    measured = jnp.clip(jnp.exp(math.log(5.0) - 3.218876 * jax.random.uniform(keys[1], (VIEWS, BRICKS, S, S * S), jnp.float32) ** block_levels(keys[1], (VIEWS, BRICKS, S, S * S), ((0, 16), (1, 16)), -0.2, 0.2)), 0.2, 5.0)
    kernel_x = jnp.clip(jnp.exp(math.log(1.0) - 1.609438 * jax.random.uniform(keys[2], (VIEWS, TAPS_XY), jnp.float32) ** block_levels(keys[2], (VIEWS, TAPS_XY), ((0, 16),), -0.2, 0.2)), 0.2, 1.0)
    kernel_y = jnp.clip(jnp.exp(math.log(1.0) - 1.609438 * jax.random.uniform(keys[3], (VIEWS, TAPS_XY), jnp.float32) ** block_levels(keys[3], (VIEWS, TAPS_XY), ((0, 16),), -0.2, 0.2)), 0.2, 1.0)
    kernel_z = jnp.clip(jnp.exp(math.log(1.0) - 1.609438 * jax.random.uniform(keys[4], (VIEWS, TAPS_Z), jnp.float32) ** block_levels(keys[4], (VIEWS, TAPS_Z), ((0, 16),), -0.2, 0.2)), 0.2, 1.0)
    neighbors = draw_neighbors(jax.random.fold_in(keys[7], 71), 0)
    inside = plant((jax.random.randint(keys[6], (BRICKS,), 0, 4) < 3).astype(jnp.int32), jax.random.fold_in(keys[6], 1), 0, 1)
    return {"estimate": estimate, "measured": measured, "kernel_x": kernel_x, "kernel_y": kernel_y, "kernel_z": kernel_z, "neighbors": neighbors, "inside": inside}


def normalized(kernel):
    return kernel / jnp.sum(kernel)


def neighbor_planes(volume, brick_ids, first_plane, radius, axis_dim):
    planes = lax.slice_in_dim(volume, first_plane, first_plane + radius, axis=axis_dim)
    chosen = jnp.take(planes, jnp.maximum(brick_ids, 0), axis=0)
    present = (brick_ids >= 0).astype(volume.dtype).reshape(-1, 1, 1, 1)
    return chosen * present


def blur_pass(volume, neighbors, kernel, axis_dim, flipped):
    radius = (kernel.shape[0] - 1) // 2
    length = volume.shape[axis_dim]
    low_side = neighbor_planes(volume, neighbors[:, 2 * axis_dim - 2], length - radius, radius, axis_dim)
    high_side = neighbor_planes(volume, neighbors[:, 2 * axis_dim - 1], 0, radius, axis_dim)
    extended = jnp.concatenate([low_side, volume, high_side], axis=axis_dim)
    summed = jnp.zeros_like(volume)
    for position in range(2 * radius + 1):
        weight = kernel[2 * radius - position] if flipped else kernel[position]
        summed = summed + weight * lax.slice_in_dim(extended, position, position + length, axis=axis_dim)
    return summed


def reference(estimate, measured, kernel_x, kernel_y, kernel_z, neighbors, inside):
    current = estimate.reshape(BRICKS, S, S, S)
    recorded_all = measured.reshape(VIEWS, BRICKS, S, S, S)
    keep_mask = (inside > 0)[:, None, None, None]
    for sweep_no in range(ITERS):
        def one_view(summed, view_items, current=current):
            recorded, along_x, along_y, along_z = view_items
            along_x = normalized(along_x)
            along_y = normalized(along_y)
            along_z = normalized(along_z)
            blurred = blur_pass(current, neighbors, along_x, 1, False)
            blurred = blur_pass(blurred, neighbors, along_y, 2, False)
            blurred = blur_pass(blurred, neighbors, along_z, 3, False)
            quotient = recorded / blurred
            spread = blur_pass(quotient, neighbors, along_z, 3, True)
            spread = blur_pass(spread, neighbors, along_y, 2, True)
            spread = blur_pass(spread, neighbors, along_x, 1, True)
            return summed + spread, None
        summed, unused = lax.scan(one_view, jnp.zeros_like(current), (recorded_all, kernel_x, kernel_y, kernel_z))
        current = current * jnp.where(keep_mask, summed / VIEWS, 1.0)
    return current.reshape(BRICKS, S, S * S)
```

```python
import jax
import jax.numpy as jnp
from jax import lax
from jax.sharding import PartitionSpec as P

ITERS = 2
ROW = 4


def normalized(kernel):
    return kernel / jnp.sum(kernel)


def xor_pairs(n, m):
    return [(i, i ^ m) for i in range(n)]


def gather_rows(row, axis, n):
    me = lax.axis_index(axis)
    buf = jnp.where(jnp.arange(n)[:, None] == me, row, jnp.zeros_like(row))
    m = 1
    while m < n:
        buf = buf + lax.ppermute(buf, axis, xor_pairs(n, m))
        m *= 2
    return buf


def route(x, dest, src_of_me, nsp):
    me = lax.axis_index("space")
    rows = nsp // ROW
    my_row, my_col = me // ROW, me % ROW
    dest_col = dest[me] % ROW
    zero = jnp.zeros_like(x)
    received = []
    for k in range(ROW):
        part = jnp.where((dest_col - my_col) % ROW == k, x, zero)
        if k:
            pairs = [(a * ROW + b, a * ROW + (b + k) % ROW) for a in range(rows) for b in range(ROW)]
            part = lax.ppermute(part, "space", pairs)
        src = my_row * ROW + (my_col - k) % ROW
        received.append((part, dest[src]))
    result = zero
    for j in range(rows):
        target = ((my_row + j) % rows) * ROW + my_col
        part = zero
        for data, d in received:
            part = jnp.where(d == target, data, part)
        if j:
            pairs = [(a * ROW + c, ((a + j) % rows) * ROW + c) for a in range(rows) for c in range(ROW)]
            part = lax.ppermute(part, "space", pairs)
        src_row = src_of_me // ROW
        result = jnp.where((my_row - src_row) % rows == j, part, result)
    return result


def convolve(extended, kernel, axis, flipped):
    radius = (kernel.shape[0] - 1) // 2
    length = extended.shape[axis] - 2 * radius
    summed = None
    for position in range(2 * radius + 1):
        weight = kernel[2 * radius - position] if flipped else kernel[position]
        term = weight * lax.slice_in_dim(extended, position, position + length, axis=axis)
        summed = term if summed is None else summed + term
    return summed


def pair_halo(volume, axis, radius, partner, is_high):
    length = volume.shape[axis]
    first = lax.slice_in_dim(volume, 0, radius, axis=axis)
    last = lax.slice_in_dim(volume, length - radius, length, axis=axis)
    send = jnp.where(is_high, first, last)
    nsp = lax.axis_size("space")
    recv = lax.ppermute(send, "space", [(i, i ^ partner) for i in range(nsp)])
    zero = jnp.zeros_like(recv)
    low = jnp.where(is_high, recv, zero)
    high = jnp.where(is_high, zero, recv)
    return jnp.concatenate([low, volume, high], axis=axis)


def z_halo(volume, axis, radius):
    length = volume.shape[axis]
    nsp = lax.axis_size("space")
    first = lax.slice_in_dim(volume, 0, radius, axis=axis)
    last = lax.slice_in_dim(volume, length - radius, length, axis=axis)
    low = lax.ppermute(last, "space", [(i, i + ROW) for i in range(nsp - ROW)])
    high = lax.ppermute(first, "space", [(i + ROW, i) for i in range(nsp - ROW)])
    return jnp.concatenate([low, volume, high], axis=axis)


RS_BITS = (1, 4, 8, 2)


def bit_axis(present, m):
    order = [8, 4, 2, 1]
    return 1 + sum(1 for b in order if b in present and order.index(b) < order.index(m))


def view_reduce_scatter(full, nv):
    me = lax.axis_index("view")
    s0, s1, s2 = full.shape
    x = full.reshape(s0, 2, 2, 2, 2, s1 // nv, s2)
    present = {8, 4, 2, 1}
    for m in RS_BITS:
        ax = bit_axis(present, m)
        x0 = lax.index_in_dim(x, 0, axis=ax, keepdims=False)
        x1 = lax.index_in_dim(x, 1, axis=ax, keepdims=False)
        mine = (me & m) != 0
        keep = jnp.where(mine, x1, x0)
        send = jnp.where(mine, x0, x1)
        x = keep + lax.ppermute(send, "view", xor_pairs(nv, m))
        present.discard(m)
    return x


def view_all_gather(share, nv):
    me = lax.axis_index("view")
    x = share
    present = set()
    for m in reversed(RS_BITS):
        recv = lax.ppermute(x, "view", xor_pairs(nv, m))
        mine = (me & m) != 0
        lo = jnp.where(mine, recv, x)
        hi = jnp.where(mine, x, recv)
        ax = bit_axis(present | {m}, m)
        x = jnp.stack([lo, hi], axis=ax)
        present.add(m)
    s0 = x.shape[0]
    return x.reshape(s0, -1, x.shape[-1])


def shards(estimate, measured, kernel_x, kernel_y, kernel_z, neighbors, inside):
    side = estimate.shape[1]
    nsp = lax.axis_size("space")
    nv = lax.axis_size("view")
    me = lax.axis_index("space")
    table = gather_rows(
        jnp.concatenate([neighbors[0], inside.astype(jnp.int32)]), "space", nsp
    )
    nbr = table[:, :6]
    inside_all = table[:, 6]
    cx = (nbr[:, 0] >= 0).astype(jnp.int32)
    cy = (nbr[:, 2] >= 0).astype(jnp.int32)
    cz = jnp.zeros_like(cx)
    cur = nbr[:, 4]
    for _ in range(nsp // ROW - 1):
        cz = cz + (cur >= 0).astype(jnp.int32)
        cur = jnp.where(cur >= 0, nbr[jnp.maximum(cur, 0), 4], -1)
    ypos = jnp.where(cy == 0, cx, 3 - cx)
    place = cz * ROW + ypos
    ids = jnp.arange(nsp, dtype=jnp.int32)
    brick_at = jnp.zeros_like(place).at[place].set(ids)
    my_brick = brick_at[me]
    keep = inside_all[my_brick] > 0
    my_x = cx[my_brick]
    my_y = cy[my_brick]

    share = estimate[0].reshape(side, estimate.shape[2] // side, side)
    share = route(share, place, my_brick, nsp)
    recorded = measured[0, 0].reshape(side, side, side)
    recorded = route(recorded, place, my_brick, nsp)

    radius_x = (kernel_x.shape[1] - 1) // 2
    radius_y = (kernel_y.shape[1] - 1) // 2
    radius_z = (kernel_z.shape[1] - 1) // 2
    along_x = normalized(kernel_x[0])
    along_y = normalized(kernel_y[0])
    along_z = normalized(kernel_z[0])
    for sweep_no in range(ITERS):
        full = view_all_gather(share, nv)
        blurred = convolve(pair_halo(full, 0, radius_x, 1, my_x == 1), along_x, 0, False)
        blurred = convolve(pair_halo(blurred, 1, radius_y, 3, my_y == 1), along_y, 1, False)
        blurred = convolve(z_halo(blurred, 2, radius_z), along_z, 2, False)
        quotient = recorded / blurred
        spread = convolve(z_halo(quotient, 2, radius_z), along_z, 2, True)
        spread = convolve(pair_halo(spread, 1, radius_y, 3, my_y == 1), along_y, 1, True)
        spread = convolve(pair_halo(spread, 0, radius_x, 1, my_x == 1), along_x, 0, True)
        summed = view_reduce_scatter(spread, nv)
        share = share * jnp.where(keep, summed / (nv * measured.shape[0]), 1.0)
    share = route(share, brick_at, place[me], nsp)
    return share.reshape(1, side, estimate.shape[2])


def solution(mesh):
    placed = (
        P("space", None, "view"),
        P("view", "space", None, None),
        P("view", None),
        P("view", None),
        P("view", None),
        P("space", None),
        P("space"),
    )
    return jax.shard_map(
        shards, mesh=mesh, in_specs=placed, out_specs=P("space", None, "view"), check_vma=False
    )
```

```python
import jax
import jax.numpy as jnp
from jax import lax
from jax.sharding import PartitionSpec as P

ITERS = 2
ROW = 4


def normalized(kernel):
    return kernel / jnp.sum(kernel)


def xor_pairs(n, m):
    return [(i, i ^ m) for i in range(n)]


def gather_rows(row, axis, n):
    me = lax.axis_index(axis)
    buf = jnp.where(jnp.arange(n)[:, None] == me, row, jnp.zeros_like(row))
    m = 1
    while m < n:
        buf = buf + lax.ppermute(buf, axis, xor_pairs(n, m))
        m *= 2
    return buf


def route(x, dest, src_of_me, nsp):
    me = lax.axis_index("space")
    rows = nsp // ROW
    my_row, my_col = me // ROW, me % ROW
    dest_col = dest[me] % ROW
    zero = jnp.zeros_like(x)
    received = []
    for k in range(ROW):
        part = jnp.where(((dest_col - my_col) % ROW == k) & (dest[me] >= 0), x, zero)
        if k:
            pairs = [(a * ROW + b, a * ROW + (b + k) % ROW) for a in range(rows) for b in range(ROW)]
            part = lax.ppermute(part, "space", pairs)
        src = my_row * ROW + (my_col - k) % ROW
        received.append((part, dest[src]))
    result = zero
    for j in range(rows):
        target = ((my_row + j) % rows) * ROW + my_col
        part = zero
        for data, d in received:
            part = jnp.where(d == target, data, part)
        if j:
            pairs = [(a * ROW + c, ((a + j) % rows) * ROW + c) for a in range(rows) for c in range(ROW)]
            part = lax.ppermute(part, "space", pairs)
        src_row = src_of_me // ROW
        result = jnp.where(((my_row - src_row) % rows == j) & (src_of_me >= 0), part, result)
    return result


def convolve(extended, kernel, axis, flipped):
    radius = (kernel.shape[0] - 1) // 2
    length = extended.shape[axis] - 2 * radius
    summed = None
    for position in range(2 * radius + 1):
        weight = kernel[2 * radius - position] if flipped else kernel[position]
        term = weight * lax.slice_in_dim(extended, position, position + length, axis=axis)
        summed = term if summed is None else summed + term
    return summed


def pair_halo(volume, axis, radius, nbr):
    length = volume.shape[axis]
    me = lax.axis_index("space")
    nsp = lax.axis_size("space")
    lo_ids = nbr[:, 2 * axis]
    partner = jnp.maximum(lo_ids, nbr[:, 2 * axis + 1])
    is_high = lo_ids[me] >= 0
    first = lax.slice_in_dim(volume, 0, radius, axis=axis)
    last = lax.slice_in_dim(volume, length - radius, length, axis=axis)
    send = jnp.where(is_high, first, last)
    recv = route(send, partner, partner[me], nsp)
    zero = jnp.zeros_like(recv)
    low = jnp.where(is_high, recv, zero)
    high = jnp.where(is_high, zero, recv)
    return jnp.concatenate([low, volume, high], axis=axis)


def z_halo(volume, axis, radius, nbr):
    length = volume.shape[axis]
    me = lax.axis_index("space")
    nsp = lax.axis_size("space")
    first = lax.slice_in_dim(volume, 0, radius, axis=axis)
    last = lax.slice_in_dim(volume, length - radius, length, axis=axis)
    low = route(last, nbr[:, 2 * axis + 1], nbr[me, 2 * axis], nsp)
    high = route(first, nbr[:, 2 * axis], nbr[me, 2 * axis + 1], nsp)
    return jnp.concatenate([low, volume, high], axis=axis)


RS_BITS = (1, 4, 8, 2)


def bit_axis(present, m):
    order = [8, 4, 2, 1]
    return 1 + sum(1 for b in order if b in present and order.index(b) < order.index(m))


def view_reduce_scatter(full, nv):
    me = lax.axis_index("view")
    s0, s1, s2 = full.shape
    x = full.reshape(s0, 2, 2, 2, 2, s1 // nv, s2)
    present = {8, 4, 2, 1}
    for m in RS_BITS:
        ax = bit_axis(present, m)
        x0 = lax.index_in_dim(x, 0, axis=ax, keepdims=False)
        x1 = lax.index_in_dim(x, 1, axis=ax, keepdims=False)
        mine = (me & m) != 0
        keep = jnp.where(mine, x1, x0)
        send = jnp.where(mine, x0, x1)
        x = keep + lax.ppermute(send, "view", xor_pairs(nv, m))
        present.discard(m)
    return x


def view_all_gather(share, nv):
    me = lax.axis_index("view")
    x = share
    present = set()
    for m in reversed(RS_BITS):
        recv = lax.ppermute(x, "view", xor_pairs(nv, m))
        mine = (me & m) != 0
        lo = jnp.where(mine, recv, x)
        hi = jnp.where(mine, x, recv)
        ax = bit_axis(present | {m}, m)
        x = jnp.stack([lo, hi], axis=ax)
        present.add(m)
    s0 = x.shape[0]
    return x.reshape(s0, -1, x.shape[-1])


def shards(estimate, measured, kernel_x, kernel_y, kernel_z, neighbors, inside):
    side = estimate.shape[1]
    nsp = lax.axis_size("space")
    nv = lax.axis_size("view")
    me = lax.axis_index("space")
    table = gather_rows(
        jnp.concatenate([neighbors[0], inside.astype(jnp.int32)]), "space", nsp
    )
    nbr = table[:, :6]
    inside_all = table[:, 6]
    keep = inside_all[me] > 0
    share = estimate[0].reshape(side, estimate.shape[2] // side, side)
    recorded = measured[0, 0].reshape(side, side, side)

    radius_x = (kernel_x.shape[1] - 1) // 2
    radius_y = (kernel_y.shape[1] - 1) // 2
    radius_z = (kernel_z.shape[1] - 1) // 2
    along_x = normalized(kernel_x[0])
    along_y = normalized(kernel_y[0])
    along_z = normalized(kernel_z[0])
    for sweep_no in range(ITERS):
        full = view_all_gather(share, nv)
        blurred = convolve(pair_halo(full, 0, radius_x, nbr), along_x, 0, False)
        blurred = convolve(pair_halo(blurred, 1, radius_y, nbr), along_y, 1, False)
        blurred = convolve(z_halo(blurred, 2, radius_z, nbr), along_z, 2, False)
        quotient = recorded / blurred
        spread = convolve(z_halo(quotient, 2, radius_z, nbr), along_z, 2, True)
        spread = convolve(pair_halo(spread, 1, radius_y, nbr), along_y, 1, True)
        spread = convolve(pair_halo(spread, 0, radius_x, nbr), along_x, 0, True)
        summed = view_reduce_scatter(spread, nv)
        share = share * jnp.where(keep, summed / (nv * measured.shape[0]), 1.0)
    return share.reshape(1, side, estimate.shape[2])


def solution(mesh):
    placed = (
        P("space", None, "view"),
        P("view", "space", None, None),
        P("view", None),
        P("view", None),
        P("view", None),
        P("space", None),
        P("space"),
    )
    return jax.shard_map(
        shards, mesh=mesh, in_specs=placed, out_specs=P("space", None, "view"), check_vma=False
    )
```

```python
import jax
import jax.numpy as jnp
from jax import lax
from jax.sharding import PartitionSpec as P

ITERS = 2
ROW = 4


def normalized(kernel):
    return kernel / jnp.sum(kernel)


def xor_pairs(n, m):
    return [(i, i ^ m) for i in range(n)]


def gather_rows(row, axis, n):
    me = lax.axis_index(axis)
    buf = jnp.where(jnp.arange(n)[:, None] == me, row, jnp.zeros_like(row))
    m = 1
    while m < n:
        buf = buf + lax.ppermute(buf, axis, xor_pairs(n, m))
        m *= 2
    return buf


def route(x, dest, src_of_me, nsp):
    me = lax.axis_index("space")
    rows = nsp // ROW
    my_row, my_col = me // ROW, me % ROW
    dest_col = dest[me] % ROW
    zero = jnp.zeros_like(x)
    received = []
    for k in range(ROW):
        part = jnp.where((dest_col - my_col) % ROW == k, x, zero)
        if k:
            pairs = [(a * ROW + b, a * ROW + (b + k) % ROW) for a in range(rows) for b in range(ROW)]
            part = lax.ppermute(part, "space", pairs)
        src = my_row * ROW + (my_col - k) % ROW
        received.append((part, dest[src]))
    result = zero
    for j in range(rows):
        target = ((my_row + j) % rows) * ROW + my_col
        part = zero
        for data, d in received:
            part = jnp.where(d == target, data, part)
        if j:
            pairs = [(a * ROW + c, ((a + j) % rows) * ROW + c) for a in range(rows) for c in range(ROW)]
            part = lax.ppermute(part, "space", pairs)
        src_row = src_of_me // ROW
        result = jnp.where((my_row - src_row) % rows == j, part, result)
    return result


def convolve(extended, kernel, axis, flipped):
    radius = (kernel.shape[0] - 1) // 2
    length = extended.shape[axis] - 2 * radius
    summed = None
    for position in range(2 * radius + 1):
        weight = kernel[2 * radius - position] if flipped else kernel[position]
        term = weight * lax.slice_in_dim(extended, position, position + length, axis=axis)
        summed = term if summed is None else summed + term
    return summed


def pair_halo(volume, axis, radius, partner, is_high):
    length = volume.shape[axis]
    first = lax.slice_in_dim(volume, 0, radius, axis=axis)
    last = lax.slice_in_dim(volume, length - radius, length, axis=axis)
    send = jnp.where(is_high, first, last)
    nsp = lax.axis_size("space")
    recv = lax.ppermute(send, "space", [(i, i ^ partner) for i in range(nsp)])
    zero = jnp.zeros_like(recv)
    low = jnp.where(is_high, recv, zero)
    high = jnp.where(is_high, zero, recv)
    return jnp.concatenate([low, volume, high], axis=axis)


def z_halo(volume, axis, radius):
    length = volume.shape[axis]
    nsp = lax.axis_size("space")
    first = lax.slice_in_dim(volume, 0, radius, axis=axis)
    last = lax.slice_in_dim(volume, length - radius, length, axis=axis)
    low = lax.ppermute(last, "space", [(i, i + ROW) for i in range(nsp - ROW)])
    high = lax.ppermute(first, "space", [(i + ROW, i) for i in range(nsp - ROW)])
    return jnp.concatenate([low, volume, high], axis=axis)


RS_BITS = (1, 4, 8, 2)


def bit_axis(present, m):
    order = [8, 4, 2, 1]
    return 1 + sum(1 for b in order if b in present and order.index(b) < order.index(m))


def view_reduce_scatter(full, nv):
    me = lax.axis_index("view")
    s0, s1, s2 = full.shape
    x = full.reshape(s0, 2, 2, 2, 2, s1 // nv, s2)
    present = {8, 4, 2, 1}
    for m in RS_BITS:
        ax = bit_axis(present, m)
        x0 = lax.index_in_dim(x, 0, axis=ax, keepdims=False)
        x1 = lax.index_in_dim(x, 1, axis=ax, keepdims=False)
        mine = (me & m) != 0
        keep = jnp.where(mine, x1, x0)
        send = jnp.where(mine, x0, x1)
        x = keep + lax.ppermute(send, "view", xor_pairs(nv, m))
        present.discard(m)
    return x


def view_all_gather(share, nv):
    me = lax.axis_index("view")
    x = share
    present = set()
    for m in reversed(RS_BITS):
        recv = lax.ppermute(x, "view", xor_pairs(nv, m))
        mine = (me & m) != 0
        lo = jnp.where(mine, recv, x)
        hi = jnp.where(mine, x, recv)
        ax = bit_axis(present | {m}, m)
        x = jnp.stack([lo, hi], axis=ax)
        present.add(m)
    s0 = x.shape[0]
    return x.reshape(s0, -1, x.shape[-1])


def shards(estimate, measured, kernel_x, kernel_y, kernel_z, neighbors, inside):
    side = estimate.shape[1]
    nsp = lax.axis_size("space")
    nv = lax.axis_size("view")
    me = lax.axis_index("space")
    table = gather_rows(
        jnp.concatenate([neighbors[0], inside.astype(jnp.int32)]), "space", nsp
    )
    nbr = table[:, :6]
    inside_all = table[:, 6]
    cx = (nbr[:, 0] >= 0).astype(jnp.int32)
    cy = (nbr[:, 2] >= 0).astype(jnp.int32)
    cz = jnp.zeros_like(cx)
    cur = nbr[:, 4]
    for _ in range(nsp // ROW - 1):
        cz = cz + (cur >= 0).astype(jnp.int32)
        cur = jnp.where(cur >= 0, nbr[jnp.maximum(cur, 0), 4], -1)
    ypos = jnp.where(cy == 0, cx, 3 - cx)
    place = cz * ROW + ypos
    ids = jnp.arange(nsp, dtype=jnp.int32)
    brick_at = jnp.zeros_like(place).at[place].set(ids)
    my_brick = brick_at[me]
    keep = inside_all[my_brick] > 0
    my_x = cx[my_brick]
    my_y = cy[my_brick]

    share = jnp.transpose(estimate[0].reshape(side, estimate.shape[2] // side, side), (2, 1, 0))
    share = route(share, place, my_brick, nsp)
    recorded = jnp.transpose(measured[0, 0].reshape(side, side, side), (2, 1, 0))
    recorded = route(recorded, place, my_brick, nsp)

    radius_x = (kernel_x.shape[1] - 1) // 2
    radius_y = (kernel_y.shape[1] - 1) // 2
    radius_z = (kernel_z.shape[1] - 1) // 2
    along_x = normalized(kernel_x[0])
    along_y = normalized(kernel_y[0])
    along_z = normalized(kernel_z[0])
    for sweep_no in range(ITERS):
        full = view_all_gather(share, nv)
        blurred = convolve(pair_halo(full, 2, radius_x, 1, my_x == 1), along_x, 2, False)
        blurred = convolve(pair_halo(blurred, 1, radius_y, 3, my_y == 1), along_y, 1, False)
        blurred = convolve(z_halo(blurred, 0, radius_z), along_z, 0, False)
        quotient = recorded / blurred
        spread = convolve(z_halo(quotient, 0, radius_z), along_z, 0, True)
        spread = convolve(pair_halo(spread, 1, radius_y, 3, my_y == 1), along_y, 1, True)
        spread = convolve(pair_halo(spread, 2, radius_x, 1, my_x == 1), along_x, 2, True)
        summed = view_reduce_scatter(spread, nv)
        share = share * jnp.where(keep, summed / (nv * measured.shape[0]), 1.0)
    share = route(share, brick_at, place[me], nsp)
    return jnp.transpose(share, (2, 1, 0)).reshape(1, side, estimate.shape[2])


def solution(mesh):
    placed = (
        P("space", None, "view"),
        P("view", "space", None, None),
        P("view", None),
        P("view", None),
        P("view", None),
        P("space", None),
        P("space"),
    )
    return jax.shard_map(
        shards, mesh=mesh, in_specs=placed, out_specs=P("space", None, "view"), check_vma=False
    )
```

```python
import jax
import jax.numpy as jnp
from jax import lax
from jax.sharding import PartitionSpec as P

ITERS = 2
ROW = 4


def normalized(kernel):
    return kernel / jnp.sum(kernel)


def xor_pairs(n, m):
    return [(i, i ^ m) for i in range(n)]


def gather_rows(row, axis, n):
    me = lax.axis_index(axis)
    buf = jnp.where(jnp.arange(n)[:, None] == me, row, jnp.zeros_like(row))
    m = 1
    while m < n:
        buf = buf + lax.ppermute(buf, axis, xor_pairs(n, m))
        m *= 2
    return buf


def route(x, dest, src_of_me, nsp):
    me = lax.axis_index("space")
    rows = nsp // ROW
    my_row, my_col = me // ROW, me % ROW
    dest_col = dest[me] % ROW
    zero = jnp.zeros_like(x)
    received = []
    for k in range(ROW):
        part = jnp.where((dest_col - my_col) % ROW == k, x, zero)
        if k:
            pairs = [(a * ROW + b, a * ROW + (b + k) % ROW) for a in range(rows) for b in range(ROW)]
            part = lax.ppermute(part, "space", pairs)
        src = my_row * ROW + (my_col - k) % ROW
        received.append((part, dest[src]))
    result = zero
    for j in range(rows):
        target = ((my_row + j) % rows) * ROW + my_col
        part = zero
        for data, d in received:
            part = jnp.where(d == target, data, part)
        if j:
            pairs = [(a * ROW + c, ((a + j) % rows) * ROW + c) for a in range(rows) for c in range(ROW)]
            part = lax.ppermute(part, "space", pairs)
        src_row = src_of_me // ROW
        result = jnp.where((my_row - src_row) % rows == j, part, result)
    return result


def convolve(extended, kernel, axis, flipped):
    radius = (kernel.shape[0] - 1) // 2
    length = extended.shape[axis] - 2 * radius
    taps = kernel[::-1] if flipped else kernel
    offset = jnp.arange(length + 2 * radius)[None, :] - jnp.arange(length)[:, None]
    band = jnp.where(
        (offset >= 0) & (offset <= 2 * radius), taps[jnp.clip(offset, 0, 2 * radius)], 0.0
    )
    hi = lax.Precision.HIGHEST
    if axis == 0:
        return jnp.einsum("ot,tab->oab", band, extended, precision=hi)
    if axis == 1:
        return jnp.einsum("ot,atb->aob", band, extended, precision=hi)
    return jnp.einsum("abt,ot->abo", extended, band, precision=hi)


def pair_halo(volume, axis, radius, partner, is_high):
    length = volume.shape[axis]
    first = lax.slice_in_dim(volume, 0, radius, axis=axis)
    last = lax.slice_in_dim(volume, length - radius, length, axis=axis)
    send = jnp.where(is_high, first, last)
    nsp = lax.axis_size("space")
    recv = lax.ppermute(send, "space", [(i, i ^ partner) for i in range(nsp)])
    zero = jnp.zeros_like(recv)
    low = jnp.where(is_high, recv, zero)
    high = jnp.where(is_high, zero, recv)
    return jnp.concatenate([low, volume, high], axis=axis)


def z_halo(volume, axis, radius):
    length = volume.shape[axis]
    nsp = lax.axis_size("space")
    first = lax.slice_in_dim(volume, 0, radius, axis=axis)
    last = lax.slice_in_dim(volume, length - radius, length, axis=axis)
    low = lax.ppermute(last, "space", [(i, i + ROW) for i in range(nsp - ROW)])
    high = lax.ppermute(first, "space", [(i + ROW, i) for i in range(nsp - ROW)])
    return jnp.concatenate([low, volume, high], axis=axis)


RS_BITS = (1, 4, 8, 2)


def bit_axis(present, m):
    order = [8, 4, 2, 1]
    return 1 + sum(1 for b in order if b in present and order.index(b) < order.index(m))


def view_reduce_scatter(full, nv):
    me = lax.axis_index("view")
    s0, s1, s2 = full.shape
    x = full.reshape(s0, 2, 2, 2, 2, s1 // nv, s2)
    present = {8, 4, 2, 1}
    for m in RS_BITS:
        ax = bit_axis(present, m)
        x0 = lax.index_in_dim(x, 0, axis=ax, keepdims=False)
        x1 = lax.index_in_dim(x, 1, axis=ax, keepdims=False)
        mine = (me & m) != 0
        keep = jnp.where(mine, x1, x0)
        send = jnp.where(mine, x0, x1)
        x = keep + lax.ppermute(send, "view", xor_pairs(nv, m))
        present.discard(m)
    return x


def view_all_gather(share, nv):
    me = lax.axis_index("view")
    x = share
    present = set()
    for m in reversed(RS_BITS):
        recv = lax.ppermute(x, "view", xor_pairs(nv, m))
        mine = (me & m) != 0
        lo = jnp.where(mine, recv, x)
        hi = jnp.where(mine, x, recv)
        ax = bit_axis(present | {m}, m)
        x = jnp.stack([lo, hi], axis=ax)
        present.add(m)
    s0 = x.shape[0]
    return x.reshape(s0, -1, x.shape[-1])


def shards(estimate, measured, kernel_x, kernel_y, kernel_z, neighbors, inside):
    side = estimate.shape[1]
    nsp = lax.axis_size("space")
    nv = lax.axis_size("view")
    me = lax.axis_index("space")
    table = gather_rows(
        jnp.concatenate([neighbors[0], inside.astype(jnp.int32)]), "space", nsp
    )
    nbr = table[:, :6]
    inside_all = table[:, 6]
    cx = (nbr[:, 0] >= 0).astype(jnp.int32)
    cy = (nbr[:, 2] >= 0).astype(jnp.int32)
    cz = jnp.zeros_like(cx)
    cur = nbr[:, 4]
    for _ in range(nsp // ROW - 1):
        cz = cz + (cur >= 0).astype(jnp.int32)
        cur = jnp.where(cur >= 0, nbr[jnp.maximum(cur, 0), 4], -1)
    ypos = jnp.where(cy == 0, cx, 3 - cx)
    place = cz * ROW + ypos
    ids = jnp.arange(nsp, dtype=jnp.int32)
    brick_at = jnp.zeros_like(place).at[place].set(ids)
    my_brick = brick_at[me]
    keep = inside_all[my_brick] > 0
    my_x = cx[my_brick]
    my_y = cy[my_brick]

    share = jnp.transpose(estimate[0].reshape(side, estimate.shape[2] // side, side), (2, 1, 0))
    share = route(share, place, my_brick, nsp)
    recorded = jnp.transpose(measured[0, 0].reshape(side, side, side), (2, 1, 0))
    recorded = route(recorded, place, my_brick, nsp)

    radius_x = (kernel_x.shape[1] - 1) // 2
    radius_y = (kernel_y.shape[1] - 1) // 2
    radius_z = (kernel_z.shape[1] - 1) // 2
    along_x = normalized(kernel_x[0])
    along_y = normalized(kernel_y[0])
    along_z = normalized(kernel_z[0])
    for sweep_no in range(ITERS):
        full = view_all_gather(share, nv)
        blurred = convolve(pair_halo(full, 2, radius_x, 1, my_x == 1), along_x, 2, False)
        blurred = convolve(pair_halo(blurred, 1, radius_y, 3, my_y == 1), along_y, 1, False)
        blurred = convolve(z_halo(blurred, 0, radius_z), along_z, 0, False)
        quotient = recorded / blurred
        spread = convolve(z_halo(quotient, 0, radius_z), along_z, 0, True)
        spread = convolve(pair_halo(spread, 1, radius_y, 3, my_y == 1), along_y, 1, True)
        spread = convolve(pair_halo(spread, 2, radius_x, 1, my_x == 1), along_x, 2, True)
        summed = view_reduce_scatter(spread, nv)
        share = share * jnp.where(keep, summed / (nv * measured.shape[0]), 1.0)
    share = route(share, brick_at, place[me], nsp)
    return jnp.transpose(share, (2, 1, 0)).reshape(1, side, estimate.shape[2])


def solution(mesh):
    placed = (
        P("space", None, "view"),
        P("view", "space", None, None),
        P("view", None),
        P("view", None),
        P("view", None),
        P("space", None),
        P("space"),
    )
    return jax.shard_map(
        shards, mesh=mesh, in_specs=placed, out_specs=P("space", None, "view"), check_vma=False
    )
```

```python
import jax
import jax.numpy as jnp
from jax import lax
from jax.sharding import PartitionSpec as P

ITERS = 2
ROW = 4


def normalized(kernel):
    return kernel / jnp.sum(kernel)


def xor_pairs(n, m):
    return [(i, i ^ m) for i in range(n)]


def gather_rows(row, axis, n):
    me = lax.axis_index(axis)
    buf = jnp.where(jnp.arange(n)[:, None] == me, row, jnp.zeros_like(row))
    m = 1
    while m < n:
        buf = buf + lax.ppermute(buf, axis, xor_pairs(n, m))
        m *= 2
    return buf


def route(x, dest, src_of_me, nsp):
    me = lax.axis_index("space")
    rows = nsp // ROW
    my_row, my_col = me // ROW, me % ROW
    dest_col = dest[me] % ROW
    zero = jnp.zeros_like(x)
    received = []
    for k in range(ROW):
        part = jnp.where((dest_col - my_col) % ROW == k, x, zero)
        if k:
            pairs = [(a * ROW + b, a * ROW + (b + k) % ROW) for a in range(rows) for b in range(ROW)]
            part = lax.ppermute(part, "space", pairs)
        src = my_row * ROW + (my_col - k) % ROW
        received.append((part, dest[src]))
    result = zero
    for j in range(rows):
        target = ((my_row + j) % rows) * ROW + my_col
        part = zero
        for data, d in received:
            part = jnp.where(d == target, data, part)
        if j:
            pairs = [(a * ROW + c, ((a + j) % rows) * ROW + c) for a in range(rows) for c in range(ROW)]
            part = lax.ppermute(part, "space", pairs)
        src_row = src_of_me // ROW
        result = jnp.where((my_row - src_row) % rows == j, part, result)
    return result


def band_matrix(kernel, length, flipped):
    radius = (kernel.shape[0] - 1) // 2
    offset = jnp.arange(length + 2 * radius)[None, :] - jnp.arange(length)[:, None]
    band = jnp.zeros(offset.shape, jnp.float32)
    for position in range(2 * radius + 1):
        weight = kernel[2 * radius - position] if flipped else kernel[position]
        band = jnp.where(offset == position, weight, band)
    return band


def convolve(extended, band, axis):
    hi = lax.Precision.HIGHEST
    if axis == 0:
        return jnp.einsum("ot,tab->oab", band, extended, precision=hi)
    if axis == 1:
        return jnp.einsum("ot,atb->aob", band, extended, precision=hi)
    return jnp.einsum("abt,ot->abo", extended, band, precision=hi)


def pair_halo(volume, axis, radius, partner, is_high):
    length = volume.shape[axis]
    first = lax.slice_in_dim(volume, 0, radius, axis=axis)
    last = lax.slice_in_dim(volume, length - radius, length, axis=axis)
    send = jnp.where(is_high, first, last)
    nsp = lax.axis_size("space")
    recv = lax.ppermute(send, "space", [(i, i ^ partner) for i in range(nsp)])
    zero = jnp.zeros_like(recv)
    low = jnp.where(is_high, recv, zero)
    high = jnp.where(is_high, zero, recv)
    return jnp.concatenate([low, volume, high], axis=axis)


def z_halo(volume, axis, radius):
    length = volume.shape[axis]
    nsp = lax.axis_size("space")
    first = lax.slice_in_dim(volume, 0, radius, axis=axis)
    last = lax.slice_in_dim(volume, length - radius, length, axis=axis)
    low = lax.ppermute(last, "space", [(i, i + ROW) for i in range(nsp - ROW)])
    high = lax.ppermute(first, "space", [(i + ROW, i) for i in range(nsp - ROW)])
    return jnp.concatenate([low, volume, high], axis=axis)


RS_BITS = (1, 4, 8, 2)


def bit_axis(present, m):
    order = [8, 4, 2, 1]
    return 1 + sum(1 for b in order if b in present and order.index(b) < order.index(m))


def view_reduce_scatter(full, nv):
    me = lax.axis_index("view")
    s0, s1, s2 = full.shape
    x = full.reshape(s0, 2, 2, 2, 2, s1 // nv, s2)
    present = {8, 4, 2, 1}
    for m in RS_BITS:
        ax = bit_axis(present, m)
        x0 = lax.index_in_dim(x, 0, axis=ax, keepdims=False)
        x1 = lax.index_in_dim(x, 1, axis=ax, keepdims=False)
        mine = (me & m) != 0
        keep = jnp.where(mine, x1, x0)
        send = jnp.where(mine, x0, x1)
        x = keep + lax.ppermute(send, "view", xor_pairs(nv, m))
        present.discard(m)
    return x


def view_all_gather(share, nv):
    me = lax.axis_index("view")
    x = share
    present = set()
    for m in reversed(RS_BITS):
        recv = lax.ppermute(x, "view", xor_pairs(nv, m))
        mine = (me & m) != 0
        lo = jnp.where(mine, recv, x)
        hi = jnp.where(mine, x, recv)
        ax = bit_axis(present | {m}, m)
        x = jnp.stack([lo, hi], axis=ax)
        present.add(m)
    s0 = x.shape[0]
    return x.reshape(s0, -1, x.shape[-1])


def shards(estimate, measured, kernel_x, kernel_y, kernel_z, neighbors, inside):
    side = estimate.shape[1]
    nsp = lax.axis_size("space")
    nv = lax.axis_size("view")
    me = lax.axis_index("space")
    table = gather_rows(
        jnp.concatenate([neighbors[0], inside.astype(jnp.int32)]), "space", nsp
    )
    nbr = table[:, :6]
    inside_all = table[:, 6]
    cx = (nbr[:, 0] >= 0).astype(jnp.int32)
    cy = (nbr[:, 2] >= 0).astype(jnp.int32)
    cz = jnp.zeros_like(cx)
    cur = nbr[:, 4]
    for _ in range(nsp // ROW - 1):
        cz = cz + (cur >= 0).astype(jnp.int32)
        cur = jnp.where(cur >= 0, nbr[jnp.maximum(cur, 0), 4], -1)
    ypos = jnp.where(cy == 0, cx, 3 - cx)
    place = cz * ROW + ypos
    ids = jnp.arange(nsp, dtype=jnp.int32)
    brick_at = jnp.zeros_like(place).at[place].set(ids)
    my_brick = brick_at[me]
    keep = inside_all[my_brick] > 0
    my_x = cx[my_brick]
    my_y = cy[my_brick]

    share = jnp.transpose(estimate[0].reshape(side, estimate.shape[2] // side, side), (2, 1, 0))
    share = route(share, place, my_brick, nsp)
    recorded = jnp.transpose(measured[0, 0].reshape(side, side, side), (2, 1, 0))
    recorded = route(recorded, place, my_brick, nsp)

    radius_x = (kernel_x.shape[1] - 1) // 2
    radius_y = (kernel_y.shape[1] - 1) // 2
    radius_z = (kernel_z.shape[1] - 1) // 2
    along_x = normalized(kernel_x[0])
    along_y = normalized(kernel_y[0])
    along_z = normalized(kernel_z[0])
    bands = {
        (axis, flipped): band_matrix(taps, side, flipped)
        for axis, taps in ((2, along_x), (1, along_y), (0, along_z))
        for flipped in (False, True)
    }
    for sweep_no in range(ITERS):
        full = view_all_gather(share, nv)
        blurred = convolve(pair_halo(full, 2, radius_x, 1, my_x == 1), bands[2, False], 2)
        blurred = convolve(pair_halo(blurred, 1, radius_y, 3, my_y == 1), bands[1, False], 1)
        blurred = convolve(z_halo(blurred, 0, radius_z), bands[0, False], 0)
        quotient = recorded / blurred
        spread = convolve(z_halo(quotient, 0, radius_z), bands[0, True], 0)
        spread = convolve(pair_halo(spread, 1, radius_y, 3, my_y == 1), bands[1, True], 1)
        spread = convolve(pair_halo(spread, 2, radius_x, 1, my_x == 1), bands[2, True], 2)
        summed = view_reduce_scatter(spread, nv)
        share = share * jnp.where(keep, summed / (nv * measured.shape[0]), 1.0)
    share = route(share, brick_at, place[me], nsp)
    return jnp.transpose(share, (2, 1, 0)).reshape(1, side, estimate.shape[2])


def solution(mesh):
    placed = (
        P("space", None, "view"),
        P("view", "space", None, None),
        P("view", None),
        P("view", None),
        P("view", None),
        P("space", None),
        P("space"),
    )
    return jax.shard_map(
        shards, mesh=mesh, in_specs=placed, out_specs=P("space", None, "view"), check_vma=False
    )
```

```python
import jax
import jax.numpy as jnp
from jax import lax
from jax.sharding import PartitionSpec as P

ITERS = 2
ROW = 4


def normalized(kernel):
    return kernel / jnp.sum(kernel)


def xor_pairs(n, m):
    return [(i, i ^ m) for i in range(n)]


def gather_rows(row, axis, n):
    me = lax.axis_index(axis)
    buf = jnp.where(jnp.arange(n)[:, None] == me, row, jnp.zeros_like(row))
    m = 1
    while m < n:
        buf = buf + lax.ppermute(buf, axis, xor_pairs(n, m))
        m *= 2
    return buf


def route(x, dest, src_of_me, nsp):
    me = lax.axis_index("space")
    rows = nsp // ROW
    my_row, my_col = me // ROW, me % ROW
    dest_col = dest[me] % ROW
    zero = jnp.zeros_like(x)
    received = []
    for k in range(ROW):
        part = jnp.where((dest_col - my_col) % ROW == k, x, zero)
        if k:
            pairs = [(a * ROW + b, a * ROW + (b + k) % ROW) for a in range(rows) for b in range(ROW)]
            part = lax.ppermute(part, "space", pairs)
        src = my_row * ROW + (my_col - k) % ROW
        received.append((part, dest[src]))
    result = zero
    for j in range(rows):
        target = ((my_row + j) % rows) * ROW + my_col
        part = zero
        for data, d in received:
            part = jnp.where(d == target, data, part)
        if j:
            pairs = [(a * ROW + c, ((a + j) % rows) * ROW + c) for a in range(rows) for c in range(ROW)]
            part = lax.ppermute(part, "space", pairs)
        src_row = src_of_me // ROW
        result = jnp.where((my_row - src_row) % rows == j, part, result)
    return result


def band_matrix(kernel, length, flipped):
    radius = (kernel.shape[0] - 1) // 2
    offset = jnp.arange(length + 2 * radius)[None, :] - jnp.arange(length)[:, None]
    band = jnp.zeros(offset.shape, jnp.float32)
    for position in range(2 * radius + 1):
        weight = kernel[2 * radius - position] if flipped else kernel[position]
        band = jnp.where(offset == position, weight, band)
    return band


def convolve(extended, band, axis):
    hi = lax.Precision.HIGHEST
    if axis == 0:
        return jnp.einsum("ot,tab->oab", band, extended, precision=hi)
    if axis == 1:
        return jnp.einsum("ot,atb->aob", band, extended, precision=hi)
    return jnp.einsum("abt,ot->abo", extended, band, precision=hi)


def pair_halo(volume, axis, radius, partner, is_high):
    length = volume.shape[axis]
    first = lax.slice_in_dim(volume, 0, radius, axis=axis)
    last = lax.slice_in_dim(volume, length - radius, length, axis=axis)
    send = jnp.where(is_high, first, last)
    nsp = lax.axis_size("space")
    recv = lax.ppermute(send, "space", [(i, i ^ partner) for i in range(nsp)])
    zero = jnp.zeros_like(recv)
    low = jnp.where(is_high, recv, zero)
    high = jnp.where(is_high, zero, recv)
    return jnp.concatenate([low, volume, high], axis=axis)


def z_halo(volume, axis, radius):
    length = volume.shape[axis]
    nsp = lax.axis_size("space")
    first = lax.slice_in_dim(volume, 0, radius, axis=axis)
    last = lax.slice_in_dim(volume, length - radius, length, axis=axis)
    low = lax.ppermute(last, "space", [(i, i + ROW) for i in range(nsp - ROW)])
    high = lax.ppermute(first, "space", [(i + ROW, i) for i in range(nsp - ROW)])
    return jnp.concatenate([low, volume, high], axis=axis)


RS_BITS = (1, 4, 8, 2)


def bit_axis(present, m):
    order = [8, 4, 2, 1]
    return 1 + sum(1 for b in order if b in present and order.index(b) < order.index(m))


def view_reduce_scatter(full, nv):
    me = lax.axis_index("view")
    s0, s1, s2 = full.shape
    x = full.reshape(s0, 2, 2, 2, 2, s1 // nv, s2)
    present = {8, 4, 2, 1}
    for m in RS_BITS:
        ax = bit_axis(present, m)
        x0 = lax.index_in_dim(x, 0, axis=ax, keepdims=False)
        x1 = lax.index_in_dim(x, 1, axis=ax, keepdims=False)
        mine = (me & m) != 0
        keep = jnp.where(mine, x1, x0)
        send = jnp.where(mine, x0, x1)
        x = keep + lax.ppermute(send, "view", xor_pairs(nv, m))
        present.discard(m)
    return x


def view_all_gather(share, nv):
    me = lax.axis_index("view")
    x = share
    present = set()
    for m in reversed(RS_BITS):
        recv = lax.ppermute(x, "view", xor_pairs(nv, m))
        mine = (me & m) != 0
        lo = jnp.where(mine, recv, x)
        hi = jnp.where(mine, x, recv)
        ax = bit_axis(present | {m}, m)
        x = jnp.stack([lo, hi], axis=ax)
        present.add(m)
    s0 = x.shape[0]
    return x.reshape(s0, -1, x.shape[-1])


def shards(estimate, measured, kernel_x, kernel_y, kernel_z, neighbors, inside):
    side = estimate.shape[1]
    nsp = lax.axis_size("space")
    nv = lax.axis_size("view")
    me = lax.axis_index("space")
    table = gather_rows(
        jnp.concatenate([neighbors[0], inside.astype(jnp.int32)]), "space", nsp
    )
    nbr = table[:, :6]
    inside_all = table[:, 6]
    cx = (nbr[:, 0] >= 0).astype(jnp.int32)
    cy = (nbr[:, 2] >= 0).astype(jnp.int32)
    cz = jnp.zeros_like(cx)
    cur = nbr[:, 4]
    for _ in range(nsp // ROW - 1):
        cz = cz + (cur >= 0).astype(jnp.int32)
        cur = jnp.where(cur >= 0, nbr[jnp.maximum(cur, 0), 4], -1)
    ypos = jnp.where(cy == 0, cx, 3 - cx)
    place = cz * ROW + ypos
    ids = jnp.arange(nsp, dtype=jnp.int32)
    brick_at = jnp.zeros_like(place).at[place].set(ids)
    my_brick = brick_at[me]
    keep = inside_all[my_brick] > 0
    my_x = cx[my_brick]
    my_y = cy[my_brick]

    share = jnp.transpose(estimate[0].reshape(side, estimate.shape[2] // side, side), (2, 1, 0))
    share = route(share, place, my_brick, nsp)
    recorded = jnp.transpose(measured[0, 0].reshape(side, side, side), (2, 1, 0))
    recorded = route(recorded, place, my_brick, nsp)

    radius_x = (kernel_x.shape[1] - 1) // 2
    radius_y = (kernel_y.shape[1] - 1) // 2
    radius_z = (kernel_z.shape[1] - 1) // 2
    along_x = normalized(kernel_x[0])
    along_y = normalized(kernel_y[0])
    along_z = normalized(kernel_z[0])
    bands = {
        (axis, flipped): band_matrix(taps, side, flipped)
        for axis, taps in ((2, along_x), (1, along_y), (0, along_z))
        for flipped in (False, True)
    }
    bands = lax.optimization_barrier(bands)
    for sweep_no in range(ITERS):
        full = view_all_gather(share, nv)
        blurred = convolve(pair_halo(full, 2, radius_x, 1, my_x == 1), bands[2, False], 2)
        blurred = convolve(pair_halo(blurred, 1, radius_y, 3, my_y == 1), bands[1, False], 1)
        blurred = convolve(z_halo(blurred, 0, radius_z), bands[0, False], 0)
        quotient = recorded / blurred
        spread = convolve(z_halo(quotient, 0, radius_z), bands[0, True], 0)
        spread = convolve(pair_halo(spread, 1, radius_y, 3, my_y == 1), bands[1, True], 1)
        spread = convolve(pair_halo(spread, 2, radius_x, 1, my_x == 1), bands[2, True], 2)
        summed = view_reduce_scatter(spread, nv)
        share = share * jnp.where(keep, summed / (nv * measured.shape[0]), 1.0)
    share = route(share, brick_at, place[me], nsp)
    return jnp.transpose(share, (2, 1, 0)).reshape(1, side, estimate.shape[2])


def solution(mesh):
    placed = (
        P("space", None, "view"),
        P("view", "space", None, None),
        P("view", None),
        P("view", None),
        P("view", None),
        P("space", None),
        P("space"),
    )
    return jax.shard_map(
        shards, mesh=mesh, in_specs=placed, out_specs=P("space", None, "view"), check_vma=False
    )
```

```python
import jax
import jax.numpy as jnp
from jax import lax
from jax.sharding import PartitionSpec as P

ITERS = 2
ROW = 4


def normalized(kernel):
    return kernel / jnp.sum(kernel)


def xor_pairs(n, m):
    return [(i, i ^ m) for i in range(n)]


def gather_rows(row, axis, n):
    me = lax.axis_index(axis)
    buf = jnp.where(jnp.arange(n)[:, None] == me, row, jnp.zeros_like(row))
    m = 1
    while m < n:
        buf = buf + lax.ppermute(buf, axis, xor_pairs(n, m))
        m *= 2
    return buf


def route(x, dest, src_of_me, nsp, columns_first=False):
    me = lax.axis_index("space")
    rows = nsp // ROW
    if columns_first:
        n1, n2 = rows, ROW
        first, second = (lambda s: s // ROW), (lambda s: s % ROW)
        put = lambda s2, s1: s1 * ROW + s2
    else:
        n1, n2 = ROW, rows
        first, second = (lambda s: s % ROW), (lambda s: s // ROW)
        put = lambda s2, s1: s2 * ROW + s1
    my1, my2 = first(me), second(me)
    dest1 = first(dest[me])
    zero = jnp.zeros_like(x)
    received = []
    for k in range(n1):
        part = jnp.where((dest1 - my1) % n1 == k, x, zero)
        if k:
            pairs = [(put(q2, q1), put(q2, (q1 + k) % n1)) for q2 in range(n2) for q1 in range(n1)]
            part = lax.ppermute(part, "space", pairs)
        received.append((part, dest[put(my2, (my1 - k) % n1)]))
    result = zero
    for j in range(n2):
        target = put((my2 + j) % n2, my1)
        part = zero
        for data, d in received:
            part = jnp.where(d == target, data, part)
        if j:
            pairs = [(put(q2, q1), put((q2 + j) % n2, q1)) for q2 in range(n2) for q1 in range(n1)]
            part = lax.ppermute(part, "space", pairs)
        result = jnp.where((my2 - second(src_of_me)) % n2 == j, part, result)
    return result


def band_matrix(kernel, length, flipped):
    radius = (kernel.shape[0] - 1) // 2
    offset = jnp.arange(length + 2 * radius)[None, :] - jnp.arange(length)[:, None]
    band = jnp.zeros(offset.shape, jnp.float32)
    for position in range(2 * radius + 1):
        weight = kernel[2 * radius - position] if flipped else kernel[position]
        band = jnp.where(offset == position, weight, band)
    return band


def convolve(extended, band, axis):
    hi = lax.Precision.HIGHEST
    if axis == 0:
        return jnp.einsum("ot,tab->oab", band, extended, precision=hi)
    if axis == 1:
        return jnp.einsum("ot,atb->aob", band, extended, precision=hi)
    return jnp.einsum("abt,ot->abo", extended, band, precision=hi)


def pair_halo(volume, axis, radius, partner, is_high):
    length = volume.shape[axis]
    first = lax.slice_in_dim(volume, 0, radius, axis=axis)
    last = lax.slice_in_dim(volume, length - radius, length, axis=axis)
    send = jnp.where(is_high, first, last)
    nsp = lax.axis_size("space")
    recv = lax.ppermute(send, "space", [(i, i ^ partner) for i in range(nsp)])
    zero = jnp.zeros_like(recv)
    low = jnp.where(is_high, recv, zero)
    high = jnp.where(is_high, zero, recv)
    return jnp.concatenate([low, volume, high], axis=axis)


def z_halo(volume, axis, radius):
    length = volume.shape[axis]
    nsp = lax.axis_size("space")
    first = lax.slice_in_dim(volume, 0, radius, axis=axis)
    last = lax.slice_in_dim(volume, length - radius, length, axis=axis)
    low = lax.ppermute(last, "space", [(i, i + ROW) for i in range(nsp - ROW)])
    high = lax.ppermute(first, "space", [(i + ROW, i) for i in range(nsp - ROW)])
    return jnp.concatenate([low, volume, high], axis=axis)


RS_BITS = (1, 4, 8, 2)


def bit_axis(present, m):
    order = [8, 4, 2, 1]
    return 1 + sum(1 for b in order if b in present and order.index(b) < order.index(m))


def view_reduce_scatter(full, nv):
    me = lax.axis_index("view")
    s0, s1, s2 = full.shape
    x = full.reshape(s0, 2, 2, 2, 2, s1 // nv, s2)
    present = {8, 4, 2, 1}
    for m in RS_BITS:
        ax = bit_axis(present, m)
        x0 = lax.index_in_dim(x, 0, axis=ax, keepdims=False)
        x1 = lax.index_in_dim(x, 1, axis=ax, keepdims=False)
        mine = (me & m) != 0
        keep = jnp.where(mine, x1, x0)
        send = jnp.where(mine, x0, x1)
        x = keep + lax.ppermute(send, "view", xor_pairs(nv, m))
        present.discard(m)
    return x


def view_all_gather(share, nv):
    me = lax.axis_index("view")
    x = share
    present = set()
    for m in reversed(RS_BITS):
        recv = lax.ppermute(x, "view", xor_pairs(nv, m))
        mine = (me & m) != 0
        lo = jnp.where(mine, recv, x)
        hi = jnp.where(mine, x, recv)
        ax = bit_axis(present | {m}, m)
        x = jnp.stack([lo, hi], axis=ax)
        present.add(m)
    s0 = x.shape[0]
    return x.reshape(s0, -1, x.shape[-1])


def shards(estimate, measured, kernel_x, kernel_y, kernel_z, neighbors, inside):
    side = estimate.shape[1]
    nsp = lax.axis_size("space")
    nv = lax.axis_size("view")
    me = lax.axis_index("space")
    table = gather_rows(
        jnp.concatenate([neighbors[0], inside.astype(jnp.int32)]), "space", nsp
    )
    nbr = table[:, :6]
    inside_all = table[:, 6]
    cx = (nbr[:, 0] >= 0).astype(jnp.int32)
    cy = (nbr[:, 2] >= 0).astype(jnp.int32)
    cz = jnp.zeros_like(cx)
    cur = nbr[:, 4]
    for _ in range(nsp // ROW - 1):
        cz = cz + (cur >= 0).astype(jnp.int32)
        cur = jnp.where(cur >= 0, nbr[jnp.maximum(cur, 0), 4], -1)
    ypos = jnp.where(cy == 0, cx, 3 - cx)
    place = cz * ROW + ypos
    ids = jnp.arange(nsp, dtype=jnp.int32)
    brick_at = jnp.zeros_like(place).at[place].set(ids)
    my_brick = brick_at[me]
    keep = inside_all[my_brick] > 0
    my_x = cx[my_brick]
    my_y = cy[my_brick]

    share = jnp.transpose(estimate[0].reshape(side, estimate.shape[2] // side, side), (2, 1, 0))
    share = route(share, place, my_brick, nsp)
    recorded = jnp.transpose(measured[0, 0].reshape(side, side, side), (2, 1, 0))
    half = side // 2
    recorded = jnp.concatenate(
        [
            route(recorded[:half], place, my_brick, nsp),
            route(recorded[half:], place, my_brick, nsp, columns_first=True),
        ],
        axis=0,
    )

    radius_x = (kernel_x.shape[1] - 1) // 2
    radius_y = (kernel_y.shape[1] - 1) // 2
    radius_z = (kernel_z.shape[1] - 1) // 2
    along_x = normalized(kernel_x[0])
    along_y = normalized(kernel_y[0])
    along_z = normalized(kernel_z[0])
    bands = {
        (axis, flipped): band_matrix(taps, side, flipped)
        for axis, taps in ((2, along_x), (1, along_y), (0, along_z))
        for flipped in (False, True)
    }
    bands = lax.optimization_barrier(bands)
    for sweep_no in range(ITERS):
        full = view_all_gather(share, nv)
        blurred = convolve(pair_halo(full, 2, radius_x, 1, my_x == 1), bands[2, False], 2)
        blurred = convolve(pair_halo(blurred, 1, radius_y, 3, my_y == 1), bands[1, False], 1)
        blurred = convolve(z_halo(blurred, 0, radius_z), bands[0, False], 0)
        quotient = recorded / blurred
        spread = convolve(z_halo(quotient, 0, radius_z), bands[0, True], 0)
        spread = convolve(pair_halo(spread, 1, radius_y, 3, my_y == 1), bands[1, True], 1)
        spread = convolve(pair_halo(spread, 2, radius_x, 1, my_x == 1), bands[2, True], 2)
        summed = view_reduce_scatter(spread, nv)
        share = share * jnp.where(keep, summed / (nv * measured.shape[0]), 1.0)
    share = route(share, brick_at, place[me], nsp)
    return jnp.transpose(share, (2, 1, 0)).reshape(1, side, estimate.shape[2])


def solution(mesh):
    placed = (
        P("space", None, "view"),
        P("view", "space", None, None),
        P("view", None),
        P("view", None),
        P("view", None),
        P("space", None),
        P("space"),
    )
    return jax.shard_map(
        shards, mesh=mesh, in_specs=placed, out_specs=P("space", None, "view"), check_vma=False
    )
```

```python
import jax
import jax.numpy as jnp
from jax import lax
from jax.sharding import PartitionSpec as P

ITERS = 2
ROW = 4


def normalized(kernel):
    return kernel / jnp.sum(kernel)


def xor_pairs(n, m):
    return [(i, i ^ m) for i in range(n)]


def gather_rows(row, axis, n):
    me = lax.axis_index(axis)
    buf = jnp.where(jnp.arange(n)[:, None] == me, row, jnp.zeros_like(row))
    m = 1
    while m < n:
        buf = buf + lax.ppermute(buf, axis, xor_pairs(n, m))
        m *= 2
    return buf


def route(x, dest, src_of_me, nsp, columns_first=False):
    me = lax.axis_index("space")
    rows = nsp // ROW
    if columns_first:
        n1, n2 = rows, ROW
        first, second = (lambda s: s // ROW), (lambda s: s % ROW)
        put = lambda s2, s1: s1 * ROW + s2
    else:
        n1, n2 = ROW, rows
        first, second = (lambda s: s % ROW), (lambda s: s // ROW)
        put = lambda s2, s1: s2 * ROW + s1
    my1, my2 = first(me), second(me)
    dest1 = first(dest[me])
    zero = jnp.zeros_like(x)
    received = []
    for k in range(n1):
        part = jnp.where((dest1 - my1) % n1 == k, x, zero)
        if k:
            pairs = [(put(q2, q1), put(q2, (q1 + k) % n1)) for q2 in range(n2) for q1 in range(n1)]
            part = lax.ppermute(part, "space", pairs)
        received.append((part, dest[put(my2, (my1 - k) % n1)]))
    result = zero
    for j in range(n2):
        target = put((my2 + j) % n2, my1)
        part = zero
        for data, d in received:
            part = jnp.where(d == target, data, part)
        if j:
            pairs = [(put(q2, q1), put((q2 + j) % n2, q1)) for q2 in range(n2) for q1 in range(n1)]
            part = lax.ppermute(part, "space", pairs)
        result = jnp.where((my2 - second(src_of_me)) % n2 == j, part, result)
    return result


def band_matrix(kernel, length, flipped):
    radius = (kernel.shape[0] - 1) // 2
    offset = jnp.arange(length + 2 * radius)[None, :] - jnp.arange(length)[:, None]
    band = jnp.zeros(offset.shape, jnp.float32)
    for position in range(2 * radius + 1):
        weight = kernel[2 * radius - position] if flipped else kernel[position]
        band = jnp.where(offset == position, weight, band)
    return band


def convolve(extended, band, axis):
    hi = lax.Precision.HIGHEST
    if axis == 0:
        return jnp.einsum("ot,tab->oab", band, extended, precision=hi)
    if axis == 1:
        return jnp.einsum("ot,atb->aob", band, extended, precision=hi)
    return jnp.einsum("abt,ot->abo", extended, band, precision=hi)


def pair_halo(volume, axis, radius, partner, is_high):
    length = volume.shape[axis]
    first = lax.slice_in_dim(volume, 0, radius, axis=axis)
    last = lax.slice_in_dim(volume, length - radius, length, axis=axis)
    send = jnp.where(is_high, first, last)
    nsp = lax.axis_size("space")
    recv = lax.ppermute(send, "space", [(i, i ^ partner) for i in range(nsp)])
    zero = jnp.zeros_like(recv)
    low = jnp.where(is_high, recv, zero)
    high = jnp.where(is_high, zero, recv)
    return jnp.concatenate([low, volume, high], axis=axis)


def z_halo(volume, axis, radius):
    length = volume.shape[axis]
    nsp = lax.axis_size("space")
    first = lax.slice_in_dim(volume, 0, radius, axis=axis)
    last = lax.slice_in_dim(volume, length - radius, length, axis=axis)
    low = lax.ppermute(last, "space", [(i, i + ROW) for i in range(nsp - ROW)])
    high = lax.ppermute(first, "space", [(i + ROW, i) for i in range(nsp - ROW)])
    return jnp.concatenate([low, volume, high], axis=axis)


GROUPS = (2, 0)


def view_reduce_scatter(full, nv):
    me = lax.axis_index("view")
    s0, s1, s2 = full.shape
    x = full.reshape(s0, 4, 4, s1 // nv, s2)
    for shift in GROUPS:
        digit = (me >> shift) & 3
        total = lax.dynamic_index_in_dim(x, digit, axis=1, keepdims=False)
        for t in (1, 2, 3):
            piece = lax.dynamic_index_in_dim(x, digit ^ t, axis=1, keepdims=False)
            total = total + lax.ppermute(piece, "view", xor_pairs(nv, t << shift))
        x = total
    return x


def view_all_gather(share, nv):
    me = lax.axis_index("view")
    x = share
    for shift in reversed(GROUPS):
        digit = (me >> shift) & 3
        pieces = [x] + [lax.ppermute(x, "view", xor_pairs(nv, t << shift)) for t in (1, 2, 3)]
        slots = []
        for q in range(4):
            offset = digit ^ q
            slot = pieces[3]
            for t in (2, 1, 0):
                slot = jnp.where(offset == t, pieces[t], slot)
            slots.append(slot)
        x = jnp.stack(slots, axis=1)
    s0 = x.shape[0]
    return x.reshape(s0, -1, x.shape[-1])


def shards(estimate, measured, kernel_x, kernel_y, kernel_z, neighbors, inside):
    side = estimate.shape[1]
    nsp = lax.axis_size("space")
    nv = lax.axis_size("view")
    me = lax.axis_index("space")
    table = gather_rows(
        jnp.concatenate([neighbors[0], inside.astype(jnp.int32)]), "space", nsp
    )
    nbr = table[:, :6]
    inside_all = table[:, 6]
    cx = (nbr[:, 0] >= 0).astype(jnp.int32)
    cy = (nbr[:, 2] >= 0).astype(jnp.int32)
    cz = jnp.zeros_like(cx)
    cur = nbr[:, 4]
    for _ in range(nsp // ROW - 1):
        cz = cz + (cur >= 0).astype(jnp.int32)
        cur = jnp.where(cur >= 0, nbr[jnp.maximum(cur, 0), 4], -1)
    ypos = jnp.where(cy == 0, cx, 3 - cx)
    place = cz * ROW + ypos
    ids = jnp.arange(nsp, dtype=jnp.int32)
    brick_at = jnp.zeros_like(place).at[place].set(ids)
    my_brick = brick_at[me]
    keep = inside_all[my_brick] > 0
    my_x = cx[my_brick]
    my_y = cy[my_brick]

    share = jnp.transpose(estimate[0].reshape(side, estimate.shape[2] // side, side), (2, 1, 0))
    share = route(share, place, my_brick, nsp)
    recorded = jnp.transpose(measured[0, 0].reshape(side, side, side), (2, 1, 0))
    half = side // 2
    recorded = jnp.concatenate(
        [
            route(recorded[:half], place, my_brick, nsp),
            route(recorded[half:], place, my_brick, nsp, columns_first=True),
        ],
        axis=0,
    )

    radius_x = (kernel_x.shape[1] - 1) // 2
    radius_y = (kernel_y.shape[1] - 1) // 2
    radius_z = (kernel_z.shape[1] - 1) // 2
    along_x = normalized(kernel_x[0])
    along_y = normalized(kernel_y[0])
    along_z = normalized(kernel_z[0])
    bands = {
        (axis, flipped): band_matrix(taps, side, flipped)
        for axis, taps in ((2, along_x), (1, along_y), (0, along_z))
        for flipped in (False, True)
    }
    bands = lax.optimization_barrier(bands)
    for sweep_no in range(ITERS):
        full = view_all_gather(share, nv)
        blurred = convolve(pair_halo(full, 2, radius_x, 1, my_x == 1), bands[2, False], 2)
        blurred = convolve(pair_halo(blurred, 1, radius_y, 3, my_y == 1), bands[1, False], 1)
        blurred = convolve(z_halo(blurred, 0, radius_z), bands[0, False], 0)
        quotient = recorded / blurred
        spread = convolve(z_halo(quotient, 0, radius_z), bands[0, True], 0)
        spread = convolve(pair_halo(spread, 1, radius_y, 3, my_y == 1), bands[1, True], 1)
        spread = convolve(pair_halo(spread, 2, radius_x, 1, my_x == 1), bands[2, True], 2)
        summed = view_reduce_scatter(spread, nv)
        share = share * jnp.where(keep, summed / (nv * measured.shape[0]), 1.0)
    share = route(share, brick_at, place[me], nsp)
    return jnp.transpose(share, (2, 1, 0)).reshape(1, side, estimate.shape[2])


def solution(mesh):
    placed = (
        P("space", None, "view"),
        P("view", "space", None, None),
        P("view", None),
        P("view", None),
        P("view", None),
        P("space", None),
        P("space"),
    )
    return jax.shard_map(
        shards, mesh=mesh, in_specs=placed, out_specs=P("space", None, "view"), check_vma=False
    )
```

```python
import jax
import jax.numpy as jnp
from jax import lax
from jax.sharding import PartitionSpec as P

ITERS = 2
ROW = 4


def normalized(kernel):
    return kernel / jnp.sum(kernel)


def xor_pairs(n, m):
    return [(i, i ^ m) for i in range(n)]


def gather_rows(row, axis, n):
    me = lax.axis_index(axis)
    buf = jnp.where(jnp.arange(n)[:, None] == me, row, jnp.zeros_like(row))
    m = 1
    while m < n:
        buf = buf + lax.ppermute(buf, axis, xor_pairs(n, m))
        m *= 2
    return buf


def route(x, dest, src_of_me, nsp, columns_first=False):
    me = lax.axis_index("space")
    rows = nsp // ROW
    if columns_first:
        n1, n2 = rows, ROW
        first, second = (lambda s: s // ROW), (lambda s: s % ROW)
        put = lambda s2, s1: s1 * ROW + s2
    else:
        n1, n2 = ROW, rows
        first, second = (lambda s: s % ROW), (lambda s: s // ROW)
        put = lambda s2, s1: s2 * ROW + s1
    my1, my2 = first(me), second(me)
    dest1 = first(dest[me])
    zero = jnp.zeros_like(x)
    received = []
    for k in range(n1):
        part = jnp.where((dest1 - my1) % n1 == k, x, zero)
        if k:
            pairs = [(put(q2, q1), put(q2, (q1 + k) % n1)) for q2 in range(n2) for q1 in range(n1)]
            part = lax.ppermute(part, "space", pairs)
        received.append((part, dest[put(my2, (my1 - k) % n1)]))
    result = zero
    for j in range(n2):
        target = put((my2 + j) % n2, my1)
        part = zero
        for data, d in received:
            part = jnp.where(d == target, data, part)
        if j:
            pairs = [(put(q2, q1), put((q2 + j) % n2, q1)) for q2 in range(n2) for q1 in range(n1)]
            part = lax.ppermute(part, "space", pairs)
        result = jnp.where((my2 - second(src_of_me)) % n2 == j, part, result)
    return result


def band_matrix(kernel, length, flipped):
    radius = (kernel.shape[0] - 1) // 2
    offset = jnp.arange(length + 2 * radius)[None, :] - jnp.arange(length)[:, None]
    band = jnp.zeros(offset.shape, jnp.float32)
    for position in range(2 * radius + 1):
        weight = kernel[2 * radius - position] if flipped else kernel[position]
        band = jnp.where(offset == position, weight, band)
    return band


def convolve(extended, band, axis):
    hi = lax.Precision.HIGHEST
    if axis == 0:
        return jnp.einsum("ot,tab->oab", band, extended, precision=hi)
    if axis == 1:
        return jnp.einsum("ot,atb->aob", band, extended, precision=hi)
    return jnp.einsum("abt,ot->abo", extended, band, precision=hi)


def pair_halo(volume, axis, radius, partner, is_high):
    length = volume.shape[axis]
    first = lax.slice_in_dim(volume, 0, radius, axis=axis)
    last = lax.slice_in_dim(volume, length - radius, length, axis=axis)
    send = jnp.where(is_high, first, last)
    nsp = lax.axis_size("space")
    recv = lax.ppermute(send, "space", [(i, i ^ partner) for i in range(nsp)])
    zero = jnp.zeros_like(recv)
    low = jnp.where(is_high, recv, zero)
    high = jnp.where(is_high, zero, recv)
    return jnp.concatenate([low, volume, high], axis=axis)


def z_halo(volume, axis, radius):
    length = volume.shape[axis]
    nsp = lax.axis_size("space")
    first = lax.slice_in_dim(volume, 0, radius, axis=axis)
    last = lax.slice_in_dim(volume, length - radius, length, axis=axis)
    low = lax.ppermute(last, "space", [(i, i + ROW) for i in range(nsp - ROW)])
    high = lax.ppermute(first, "space", [(i + ROW, i) for i in range(nsp - ROW)])
    return jnp.concatenate([low, volume, high], axis=axis)


RS_BITS = (1, 4, 8, 2)


def bit_axis(present, m):
    order = [8, 4, 2, 1]
    return 1 + sum(1 for b in order if b in present and order.index(b) < order.index(m))


def view_reduce_scatter(full, nv):
    me = lax.axis_index("view")
    s0, s1, s2 = full.shape
    x = full.reshape(s0, 2, 2, 2, 2, s1 // nv, s2)
    present = {8, 4, 2, 1}
    for m in RS_BITS:
        ax = bit_axis(present, m)
        x0 = lax.index_in_dim(x, 0, axis=ax, keepdims=False)
        x1 = lax.index_in_dim(x, 1, axis=ax, keepdims=False)
        mine = (me & m) != 0
        keep = jnp.where(mine, x1, x0)
        send = jnp.where(mine, x0, x1)
        x = keep + lax.ppermute(send, "view", xor_pairs(nv, m))
        present.discard(m)
    return x


def view_all_gather(share, nv):
    me = lax.axis_index("view")
    x = share
    present = set()
    for m in reversed(RS_BITS):
        recv = lax.ppermute(x, "view", xor_pairs(nv, m))
        mine = (me & m) != 0
        lo = jnp.where(mine, recv, x)
        hi = jnp.where(mine, x, recv)
        ax = bit_axis(present | {m}, m)
        x = jnp.stack([lo, hi], axis=ax)
        present.add(m)
    s0 = x.shape[0]
    return x.reshape(s0, -1, x.shape[-1])


def shards(estimate, measured, kernel_x, kernel_y, kernel_z, neighbors, inside):
    side = estimate.shape[1]
    nsp = lax.axis_size("space")
    nv = lax.axis_size("view")
    me = lax.axis_index("space")
    table = gather_rows(
        jnp.concatenate([neighbors[0], inside.astype(jnp.int32)]), "space", nsp
    )
    nbr = table[:, :6]
    inside_all = table[:, 6]
    cx = (nbr[:, 0] >= 0).astype(jnp.int32)
    cy = (nbr[:, 2] >= 0).astype(jnp.int32)
    cz = jnp.zeros_like(cx)
    cur = nbr[:, 4]
    for _ in range(nsp // ROW - 1):
        cz = cz + (cur >= 0).astype(jnp.int32)
        cur = jnp.where(cur >= 0, nbr[jnp.maximum(cur, 0), 4], -1)
    ypos = jnp.where(cy == 0, cx, 3 - cx)
    place = cz * ROW + ypos
    ids = jnp.arange(nsp, dtype=jnp.int32)
    brick_at = jnp.zeros_like(place).at[place].set(ids)
    my_brick = brick_at[me]
    keep = inside_all[my_brick] > 0
    my_x = cx[my_brick]
    my_y = cy[my_brick]

    share = jnp.transpose(estimate[0].reshape(side, estimate.shape[2] // side, side), (2, 1, 0))
    share = route(share, place, my_brick, nsp)
    recorded = jnp.transpose(measured[0, 0].reshape(side, side, side), (2, 1, 0))
    chunk = side // 4
    recorded = jnp.concatenate(
        [
            route(recorded[c * chunk:(c + 1) * chunk], place, my_brick, nsp, columns_first=c % 2 == 1)
            for c in range(4)
        ],
        axis=0,
    )

    radius_x = (kernel_x.shape[1] - 1) // 2
    radius_y = (kernel_y.shape[1] - 1) // 2
    radius_z = (kernel_z.shape[1] - 1) // 2
    along_x = normalized(kernel_x[0])
    along_y = normalized(kernel_y[0])
    along_z = normalized(kernel_z[0])
    bands = {
        (axis, flipped): band_matrix(taps, side, flipped)
        for axis, taps in ((2, along_x), (1, along_y), (0, along_z))
        for flipped in (False, True)
    }
    bands = lax.optimization_barrier(bands)
    for sweep_no in range(ITERS):
        full = view_all_gather(share, nv)
        blurred = convolve(pair_halo(full, 2, radius_x, 1, my_x == 1), bands[2, False], 2)
        blurred = convolve(pair_halo(blurred, 1, radius_y, 3, my_y == 1), bands[1, False], 1)
        blurred = convolve(z_halo(blurred, 0, radius_z), bands[0, False], 0)
        quotient = recorded / blurred
        spread = convolve(z_halo(quotient, 0, radius_z), bands[0, True], 0)
        spread = convolve(pair_halo(spread, 1, radius_y, 3, my_y == 1), bands[1, True], 1)
        spread = convolve(pair_halo(spread, 2, radius_x, 1, my_x == 1), bands[2, True], 2)
        summed = view_reduce_scatter(spread, nv)
        share = share * jnp.where(keep, summed / (nv * measured.shape[0]), 1.0)
    share = route(share, brick_at, place[me], nsp)
    return jnp.transpose(share, (2, 1, 0)).reshape(1, side, estimate.shape[2])


def solution(mesh):
    placed = (
        P("space", None, "view"),
        P("view", "space", None, None),
        P("view", None),
        P("view", None),
        P("view", None),
        P("space", None),
        P("space"),
    )
    return jax.shard_map(
        shards, mesh=mesh, in_specs=placed, out_specs=P("space", None, "view"), check_vma=False
    )
```

```python
import jax
import jax.numpy as jnp
from jax import lax
from jax.sharding import PartitionSpec as P

ITERS = 2
ROW = 4


def normalized(kernel):
    return kernel / jnp.sum(kernel)


def xor_pairs(n, m):
    return [(i, i ^ m) for i in range(n)]


def gather_rows(row, axis, n):
    me = lax.axis_index(axis)
    buf = jnp.where(jnp.arange(n)[:, None] == me, row, jnp.zeros_like(row))
    m = 1
    while m < n:
        buf = buf + lax.ppermute(buf, axis, xor_pairs(n, m))
        m *= 2
    return buf


def route(x, dest, src_of_me, nsp, columns_first=False):
    me = lax.axis_index("space")
    rows = nsp // ROW
    if columns_first:
        n1, n2 = rows, ROW
        first, second = (lambda s: s // ROW), (lambda s: s % ROW)
        put = lambda s2, s1: s1 * ROW + s2
    else:
        n1, n2 = ROW, rows
        first, second = (lambda s: s % ROW), (lambda s: s // ROW)
        put = lambda s2, s1: s2 * ROW + s1
    my1, my2 = first(me), second(me)
    dest1 = first(dest[me])
    zero = jnp.zeros_like(x)
    received = []
    for k in range(n1):
        part = jnp.where((dest1 - my1) % n1 == k, x, zero)
        if k:
            pairs = [(put(q2, q1), put(q2, (q1 + k) % n1)) for q2 in range(n2) for q1 in range(n1)]
            part = lax.ppermute(part, "space", pairs)
        received.append((part, dest[put(my2, (my1 - k) % n1)]))
    result = zero
    for j in range(n2):
        target = put((my2 + j) % n2, my1)
        part = zero
        for data, d in received:
            part = jnp.where(d == target, data, part)
        if j:
            pairs = [(put(q2, q1), put((q2 + j) % n2, q1)) for q2 in range(n2) for q1 in range(n1)]
            part = lax.ppermute(part, "space", pairs)
        result = jnp.where((my2 - second(src_of_me)) % n2 == j, part, result)
    return result


def band_matrix(kernel, length, flipped):
    radius = (kernel.shape[0] - 1) // 2
    offset = jnp.arange(length + 2 * radius)[None, :] - jnp.arange(length)[:, None]
    band = jnp.zeros(offset.shape, jnp.float32)
    for position in range(2 * radius + 1):
        weight = kernel[2 * radius - position] if flipped else kernel[position]
        band = jnp.where(offset == position, weight, band)
    return band


def convolve(extended, band, axis):
    hi = lax.Precision.HIGHEST
    if axis == 0:
        return jnp.einsum("ot,tab->oab", band, extended, precision=hi)
    if axis == 1:
        return jnp.einsum("ot,atb->aob", band, extended, precision=hi)
    return jnp.einsum("abt,ot->abo", extended, band, precision=hi)


def pair_halo(volume, axis, radius, partner, is_high):
    length = volume.shape[axis]
    first = lax.slice_in_dim(volume, 0, radius, axis=axis)
    last = lax.slice_in_dim(volume, length - radius, length, axis=axis)
    send = jnp.where(is_high, first, last)
    nsp = lax.axis_size("space")
    recv = lax.ppermute(send, "space", [(i, i ^ partner) for i in range(nsp)])
    zero = jnp.zeros_like(recv)
    low = jnp.where(is_high, recv, zero)
    high = jnp.where(is_high, zero, recv)
    return jnp.concatenate([low, volume, high], axis=axis)


def xy_halo(volume, radius_i, radius_j, high_x, high_y):
    nsp = lax.axis_size("space")
    length = volume.shape[1]

    def toward(slab, axis, is_high):
        radius = radius_i if axis == 2 else radius_j
        first = lax.slice_in_dim(slab, 0, radius, axis=axis)
        last = lax.slice_in_dim(slab, length - radius, length, axis=axis)
        return jnp.where(is_high, first, last)

    def swap(x, partner):
        return lax.ppermute(x, "space", [(i, i ^ partner) for i in range(nsp)])

    def place(inner, halo, axis, is_high):
        zero = jnp.zeros_like(halo)
        low = jnp.where(is_high, halo, zero)
        high = jnp.where(is_high, zero, halo)
        return jnp.concatenate([low, inner, high], axis=axis)

    x_slab = swap(toward(volume, 2, high_x), 1)
    y_slab = swap(toward(volume, 1, high_y), 3)
    corner = swap(toward(toward(volume, 2, high_x), 1, high_y), 2)
    rows = place(volume, x_slab, 2, high_x)
    edge = place(y_slab, corner, 2, high_x)
    return place(rows, edge, 1, high_y)


def z_halo(volume, axis, radius):
    length = volume.shape[axis]
    nsp = lax.axis_size("space")
    first = lax.slice_in_dim(volume, 0, radius, axis=axis)
    last = lax.slice_in_dim(volume, length - radius, length, axis=axis)
    low = lax.ppermute(last, "space", [(i, i + ROW) for i in range(nsp - ROW)])
    high = lax.ppermute(first, "space", [(i + ROW, i) for i in range(nsp - ROW)])
    return jnp.concatenate([low, volume, high], axis=axis)


RS_BITS = (1, 4, 8, 2)


def bit_axis(present, m):
    order = [8, 4, 2, 1]
    return 1 + sum(1 for b in order if b in present and order.index(b) < order.index(m))


def view_reduce_scatter(full, nv):
    me = lax.axis_index("view")
    s0, s1, s2 = full.shape
    x = full.reshape(s0, 2, 2, 2, 2, s1 // nv, s2)
    present = {8, 4, 2, 1}
    for m in RS_BITS:
        ax = bit_axis(present, m)
        x0 = lax.index_in_dim(x, 0, axis=ax, keepdims=False)
        x1 = lax.index_in_dim(x, 1, axis=ax, keepdims=False)
        mine = (me & m) != 0
        keep = jnp.where(mine, x1, x0)
        send = jnp.where(mine, x0, x1)
        x = keep + lax.ppermute(send, "view", xor_pairs(nv, m))
        present.discard(m)
    return x


def view_all_gather(share, nv):
    me = lax.axis_index("view")
    x = share
    present = set()
    for m in reversed(RS_BITS):
        recv = lax.ppermute(x, "view", xor_pairs(nv, m))
        mine = (me & m) != 0
        lo = jnp.where(mine, recv, x)
        hi = jnp.where(mine, x, recv)
        ax = bit_axis(present | {m}, m)
        x = jnp.stack([lo, hi], axis=ax)
        present.add(m)
    s0 = x.shape[0]
    return x.reshape(s0, -1, x.shape[-1])


def shards(estimate, measured, kernel_x, kernel_y, kernel_z, neighbors, inside):
    side = estimate.shape[1]
    nsp = lax.axis_size("space")
    nv = lax.axis_size("view")
    me = lax.axis_index("space")
    table = gather_rows(
        jnp.concatenate([neighbors[0], inside.astype(jnp.int32)]), "space", nsp
    )
    nbr = table[:, :6]
    inside_all = table[:, 6]
    cx = (nbr[:, 0] >= 0).astype(jnp.int32)
    cy = (nbr[:, 2] >= 0).astype(jnp.int32)
    cz = jnp.zeros_like(cx)
    cur = nbr[:, 4]
    for _ in range(nsp // ROW - 1):
        cz = cz + (cur >= 0).astype(jnp.int32)
        cur = jnp.where(cur >= 0, nbr[jnp.maximum(cur, 0), 4], -1)
    ypos = jnp.where(cy == 0, cx, 3 - cx)
    place = cz * ROW + ypos
    ids = jnp.arange(nsp, dtype=jnp.int32)
    brick_at = jnp.zeros_like(place).at[place].set(ids)
    my_brick = brick_at[me]
    keep = inside_all[my_brick] > 0
    my_x = cx[my_brick]
    my_y = cy[my_brick]

    share = jnp.transpose(estimate[0].reshape(side, estimate.shape[2] // side, side), (2, 1, 0))
    share = route(share, place, my_brick, nsp)
    recorded = jnp.transpose(measured[0, 0].reshape(side, side, side), (2, 1, 0))
    chunk = side // 4
    recorded = jnp.concatenate(
        [
            route(recorded[c * chunk:(c + 1) * chunk], place, my_brick, nsp, columns_first=c % 2 == 1)
            for c in range(4)
        ],
        axis=0,
    )

    radius_x = (kernel_x.shape[1] - 1) // 2
    radius_y = (kernel_y.shape[1] - 1) // 2
    radius_z = (kernel_z.shape[1] - 1) // 2
    along_x = normalized(kernel_x[0])
    along_y = normalized(kernel_y[0])
    along_z = normalized(kernel_z[0])
    bands = {
        (axis, flipped): band_matrix(taps, side, flipped)
        for axis, taps in ((2, along_x), (1, along_y), (0, along_z))
        for flipped in (False, True)
    }
    bands = lax.optimization_barrier(bands)
    for sweep_no in range(ITERS):
        full = view_all_gather(share, nv)
        blurred = convolve(xy_halo(full, radius_x, radius_y, my_x == 1, my_y == 1), bands[2, False], 2)
        blurred = convolve(blurred, bands[1, False], 1)
        blurred = convolve(z_halo(blurred, 0, radius_z), bands[0, False], 0)
        quotient = recorded / blurred
        spread = convolve(z_halo(quotient, 0, radius_z), bands[0, True], 0)
        spread = convolve(xy_halo(spread, radius_x, radius_y, my_x == 1, my_y == 1), bands[1, True], 1)
        spread = convolve(spread, bands[2, True], 2)
        summed = view_reduce_scatter(spread, nv)
        share = share * jnp.where(keep, summed / (nv * measured.shape[0]), 1.0)
    share = route(share, brick_at, place[me], nsp)
    return jnp.transpose(share, (2, 1, 0)).reshape(1, side, estimate.shape[2])


def solution(mesh):
    placed = (
        P("space", None, "view"),
        P("view", "space", None, None),
        P("view", None),
        P("view", None),
        P("view", None),
        P("space", None),
        P("space"),
    )
    return jax.shard_map(
        shards, mesh=mesh, in_specs=placed, out_specs=P("space", None, "view"), check_vma=False
    )
```

```python
import jax
import jax.numpy as jnp
from jax import lax
from jax.sharding import PartitionSpec as P

ITERS = 2
ROW = 4


def normalized(kernel):
    return kernel / jnp.sum(kernel)


def xor_pairs(n, m):
    return [(i, i ^ m) for i in range(n)]


def gather_rows(row, axis, n):
    me = lax.axis_index(axis)
    buf = jnp.where(jnp.arange(n)[:, None] == me, row, jnp.zeros_like(row))
    m = 1
    while m < n:
        buf = buf + lax.ppermute(buf, axis, xor_pairs(n, m))
        m *= 2
    return buf


def route(x, dest, src_of_me, nsp, columns_first=False):
    me = lax.axis_index("space")
    rows = nsp // ROW
    if columns_first:
        n1, n2 = rows, ROW
        first, second = (lambda s: s // ROW), (lambda s: s % ROW)
        put = lambda s2, s1: s1 * ROW + s2
    else:
        n1, n2 = ROW, rows
        first, second = (lambda s: s % ROW), (lambda s: s // ROW)
        put = lambda s2, s1: s2 * ROW + s1
    my1, my2 = first(me), second(me)
    dest1 = first(dest[me])
    zero = jnp.zeros_like(x)
    received = []
    for k in range(n1):
        part = jnp.where((dest1 - my1) % n1 == k, x, zero)
        if k:
            pairs = [(put(q2, q1), put(q2, (q1 + k) % n1)) for q2 in range(n2) for q1 in range(n1)]
            part = lax.ppermute(part, "space", pairs)
        received.append((part, dest[put(my2, (my1 - k) % n1)]))
    result = zero
    for j in range(n2):
        target = put((my2 + j) % n2, my1)
        part = zero
        for data, d in received:
            part = jnp.where(d == target, data, part)
        if j:
            pairs = [(put(q2, q1), put((q2 + j) % n2, q1)) for q2 in range(n2) for q1 in range(n1)]
            part = lax.ppermute(part, "space", pairs)
        result = jnp.where((my2 - second(src_of_me)) % n2 == j, part, result)
    return result


def band_matrix(kernel, length, flipped):
    radius = (kernel.shape[0] - 1) // 2
    offset = jnp.arange(length + 2 * radius)[None, :] - jnp.arange(length)[:, None]
    band = jnp.zeros(offset.shape, jnp.float32)
    for position in range(2 * radius + 1):
        weight = kernel[2 * radius - position] if flipped else kernel[position]
        band = jnp.where(offset == position, weight, band)
    return band


def convolve(extended, band, axis):
    hi = lax.Precision.HIGHEST
    if axis == 0:
        return jnp.einsum("ot,tab->oab", band, extended, precision=hi)
    if axis == 1:
        return jnp.einsum("ot,atb->aob", band, extended, precision=hi)
    return jnp.einsum("abt,ot->abo", extended, band, precision=hi)


def pair_halo(volume, axis, radius, partner, is_high):
    length = volume.shape[axis]
    first = lax.slice_in_dim(volume, 0, radius, axis=axis)
    last = lax.slice_in_dim(volume, length - radius, length, axis=axis)
    send = jnp.where(is_high, first, last)
    nsp = lax.axis_size("space")
    recv = lax.ppermute(send, "space", [(i, i ^ partner) for i in range(nsp)])
    zero = jnp.zeros_like(recv)
    low = jnp.where(is_high, recv, zero)
    high = jnp.where(is_high, zero, recv)
    return jnp.concatenate([low, volume, high], axis=axis)


def xy_halo(volume, radius_i, radius_j, high_x, high_y):
    nsp = lax.axis_size("space")
    length = volume.shape[1]

    def toward(slab, axis, is_high):
        radius = radius_i if axis == 2 else radius_j
        first = lax.slice_in_dim(slab, 0, radius, axis=axis)
        last = lax.slice_in_dim(slab, length - radius, length, axis=axis)
        return jnp.where(is_high, first, last)

    def swap(x, partner):
        return lax.ppermute(x, "space", [(i, i ^ partner) for i in range(nsp)])

    def place(inner, halo, axis, is_high):
        zero = jnp.zeros_like(halo)
        low = jnp.where(is_high, halo, zero)
        high = jnp.where(is_high, zero, halo)
        return jnp.concatenate([low, inner, high], axis=axis)

    x_slab = swap(toward(volume, 2, high_x), 1)
    y_slab = swap(toward(volume, 1, high_y), 3)
    corner = swap(toward(toward(volume, 2, high_x), 1, high_y), 2)
    rows = place(volume, x_slab, 2, high_x)
    edge = place(y_slab, corner, 2, high_x)
    return place(rows, edge, 1, high_y)


def z_halo(volume, axis, radius):
    length = volume.shape[axis]
    nsp = lax.axis_size("space")
    first = lax.slice_in_dim(volume, 0, radius, axis=axis)
    last = lax.slice_in_dim(volume, length - radius, length, axis=axis)
    low = lax.ppermute(last, "space", [(i, i + ROW) for i in range(nsp - ROW)])
    high = lax.ppermute(first, "space", [(i + ROW, i) for i in range(nsp - ROW)])
    return jnp.concatenate([low, volume, high], axis=axis)


RS_BITS = (1, 4, 8, 2)


def bit_axis(present, m):
    order = [8, 4, 2, 1]
    return 1 + sum(1 for b in order if b in present and order.index(b) < order.index(m))


def view_reduce_scatter(x, nv, bits, present):
    me = lax.axis_index("view")
    for m in bits:
        ax = bit_axis(present, m)
        x0 = lax.index_in_dim(x, 0, axis=ax, keepdims=False)
        x1 = lax.index_in_dim(x, 1, axis=ax, keepdims=False)
        mine = (me & m) != 0
        keep = jnp.where(mine, x1, x0)
        send = jnp.where(mine, x0, x1)
        x = keep + lax.ppermute(send, "view", xor_pairs(nv, m))
        present = present - {m}
    return x, present


def view_all_gather(x, nv, bits, present):
    me = lax.axis_index("view")
    for m in bits:
        recv = lax.ppermute(x, "view", xor_pairs(nv, m))
        mine = (me & m) != 0
        lo = jnp.where(mine, recv, x)
        hi = jnp.where(mine, x, recv)
        present = present | {m}
        x = jnp.stack([lo, hi], axis=bit_axis(present, m))
    return x, present


def own_rows(x, bits, present):
    me = lax.axis_index("view")
    for m in bits:
        x = lax.dynamic_index_in_dim(x, (me & m) // m, axis=bit_axis(present, m), keepdims=False)
        present = present - {m}
    return x


def shards(estimate, measured, kernel_x, kernel_y, kernel_z, neighbors, inside):
    side = estimate.shape[1]
    nsp = lax.axis_size("space")
    nv = lax.axis_size("view")
    me = lax.axis_index("space")
    table = gather_rows(
        jnp.concatenate([neighbors[0], inside.astype(jnp.int32)]), "space", nsp
    )
    nbr = table[:, :6]
    inside_all = table[:, 6]
    cx = (nbr[:, 0] >= 0).astype(jnp.int32)
    cy = (nbr[:, 2] >= 0).astype(jnp.int32)
    cz = jnp.zeros_like(cx)
    cur = nbr[:, 4]
    for _ in range(nsp // ROW - 1):
        cz = cz + (cur >= 0).astype(jnp.int32)
        cur = jnp.where(cur >= 0, nbr[jnp.maximum(cur, 0), 4], -1)
    ypos = jnp.where(cy == 0, cx, 3 - cx)
    place = cz * ROW + ypos
    ids = jnp.arange(nsp, dtype=jnp.int32)
    brick_at = jnp.zeros_like(place).at[place].set(ids)
    my_brick = brick_at[me]
    keep = inside_all[my_brick] > 0
    my_x = cx[my_brick]
    my_y = cy[my_brick]

    share = jnp.transpose(estimate[0].reshape(side, estimate.shape[2] // side, side), (2, 1, 0))
    share = route(share, place, my_brick, nsp)
    recorded = jnp.transpose(measured[0, 0].reshape(side, side, side), (2, 1, 0))
    chunk = side // 4
    recorded = jnp.concatenate(
        [
            route(recorded[c * chunk:(c + 1) * chunk], place, my_brick, nsp, columns_first=c % 2 == 1)
            for c in range(4)
        ],
        axis=0,
    )

    radius_x = (kernel_x.shape[1] - 1) // 2
    radius_y = (kernel_y.shape[1] - 1) // 2
    radius_z = (kernel_z.shape[1] - 1) // 2
    along_x = normalized(kernel_x[0])
    along_y = normalized(kernel_y[0])
    along_z = normalized(kernel_z[0])
    bands = {
        (axis, flipped): band_matrix(taps, side, flipped)
        for axis, taps in ((2, along_x), (1, along_y), (0, along_z))
        for flipped in (False, True)
    }
    bands = lax.optimization_barrier(bands)
    views = nv * measured.shape[0]
    all_bits = {8, 4, 2, 1}
    split = lambda a: a.reshape(a.shape[0], 2, 2, 2, 2, a.shape[1] // nv, a.shape[2])
    joined = lambda a: a.reshape(a.shape[0], -1, a.shape[-1])
    full, _ = view_all_gather(share, nv, tuple(reversed(RS_BITS)), set())
    full = joined(full)
    for sweep_no in range(ITERS):
        blurred = convolve(xy_halo(full, radius_x, radius_y, my_x == 1, my_y == 1), bands[2, False], 2)
        blurred = convolve(blurred, bands[1, False], 1)
        blurred = convolve(z_halo(blurred, 0, radius_z), bands[0, False], 0)
        quotient = recorded / blurred
        spread = convolve(z_halo(quotient, 0, radius_z), bands[0, True], 0)
        spread = convolve(xy_halo(spread, radius_x, radius_y, my_x == 1, my_y == 1), bands[1, True], 1)
        spread = convolve(spread, bands[2, True], 2)
        if sweep_no == ITERS - 1:
            summed, _ = view_reduce_scatter(split(spread), nv, RS_BITS, all_bits)
            share = share * jnp.where(keep, summed / views, 1.0)
        else:
            summed, present = view_reduce_scatter(split(spread), nv, RS_BITS[:2], all_bits)
            for m in RS_BITS[2:]:
                summed = summed + lax.ppermute(summed, "view", xor_pairs(nv, m))
            quarter = own_rows(split(full), RS_BITS[:2], all_bits)
            quarter = quarter * jnp.where(keep, summed / views, 1.0)
            share = own_rows(quarter, RS_BITS[2:], present)
            full, _ = view_all_gather(quarter, nv, tuple(reversed(RS_BITS[:2])), present)
            full = joined(full)
    share = route(share, brick_at, place[me], nsp)
    return jnp.transpose(share, (2, 1, 0)).reshape(1, side, estimate.shape[2])


def solution(mesh):
    placed = (
        P("space", None, "view"),
        P("view", "space", None, None),
        P("view", None),
        P("view", None),
        P("view", None),
        P("space", None),
        P("space"),
    )
    return jax.shard_map(
        shards, mesh=mesh, in_specs=placed, out_specs=P("space", None, "view"), check_vma=False
    )
```

```python
import jax
import jax.numpy as jnp
from jax import lax
from jax.sharding import PartitionSpec as P

ITERS = 2
ROW = 4


def normalized(kernel):
    return kernel / jnp.sum(kernel)


def xor_pairs(n, m):
    return [(i, i ^ m) for i in range(n)]


def gather_rows(row, axis, n):
    me = lax.axis_index(axis)
    buf = jnp.where(jnp.arange(n)[:, None] == me, row, jnp.zeros_like(row))
    for shift in (0, 2):
        step = [lax.ppermute(buf, axis, xor_pairs(n, t << shift)) for t in (1, 2, 3)]
        buf = buf + step[0] + step[1] + step[2]
    return buf


def route(x, dest, src_of_me, nsp, columns_first=False):
    me = lax.axis_index("space")
    rows = nsp // ROW
    if columns_first:
        n1, n2 = rows, ROW
        first, second = (lambda s: s // ROW), (lambda s: s % ROW)
        put = lambda s2, s1: s1 * ROW + s2
    else:
        n1, n2 = ROW, rows
        first, second = (lambda s: s % ROW), (lambda s: s // ROW)
        put = lambda s2, s1: s2 * ROW + s1
    my1, my2 = first(me), second(me)
    dest1 = first(dest[me])
    zero = jnp.zeros_like(x)
    received = []
    for k in range(n1):
        part = jnp.where((dest1 - my1) % n1 == k, x, zero)
        if k:
            pairs = [(put(q2, q1), put(q2, (q1 + k) % n1)) for q2 in range(n2) for q1 in range(n1)]
            part = lax.ppermute(part, "space", pairs)
        received.append((part, dest[put(my2, (my1 - k) % n1)]))
    result = zero
    for j in range(n2):
        target = put((my2 + j) % n2, my1)
        part = zero
        for data, d in received:
            part = jnp.where(d == target, data, part)
        if j:
            pairs = [(put(q2, q1), put((q2 + j) % n2, q1)) for q2 in range(n2) for q1 in range(n1)]
            part = lax.ppermute(part, "space", pairs)
        result = jnp.where((my2 - second(src_of_me)) % n2 == j, part, result)
    return result


def band_matrix(kernel, length, flipped):
    radius = (kernel.shape[0] - 1) // 2
    offset = jnp.arange(length + 2 * radius)[None, :] - jnp.arange(length)[:, None]
    band = jnp.zeros(offset.shape, jnp.float32)
    for position in range(2 * radius + 1):
        weight = kernel[2 * radius - position] if flipped else kernel[position]
        band = jnp.where(offset == position, weight, band)
    return band


def convolve(extended, band, axis):
    hi = lax.Precision.HIGHEST
    if axis == 0:
        return jnp.einsum("ot,tab->oab", band, extended, precision=hi)
    if axis == 1:
        return jnp.einsum("ot,atb->aob", band, extended, precision=hi)
    return jnp.einsum("abt,ot->abo", extended, band, precision=hi)


def pair_halo(volume, axis, radius, partner, is_high):
    length = volume.shape[axis]
    first = lax.slice_in_dim(volume, 0, radius, axis=axis)
    last = lax.slice_in_dim(volume, length - radius, length, axis=axis)
    send = jnp.where(is_high, first, last)
    nsp = lax.axis_size("space")
    recv = lax.ppermute(send, "space", [(i, i ^ partner) for i in range(nsp)])
    zero = jnp.zeros_like(recv)
    low = jnp.where(is_high, recv, zero)
    high = jnp.where(is_high, zero, recv)
    return jnp.concatenate([low, volume, high], axis=axis)


def xy_halo(volume, radius_i, radius_j, high_x, high_y):
    nsp = lax.axis_size("space")
    length = volume.shape[1]

    def toward(slab, axis, is_high):
        radius = radius_i if axis == 2 else radius_j
        first = lax.slice_in_dim(slab, 0, radius, axis=axis)
        last = lax.slice_in_dim(slab, length - radius, length, axis=axis)
        return jnp.where(is_high, first, last)

    def swap(x, partner):
        return lax.ppermute(x, "space", [(i, i ^ partner) for i in range(nsp)])

    def place(inner, halo, axis, is_high):
        zero = jnp.zeros_like(halo)
        low = jnp.where(is_high, halo, zero)
        high = jnp.where(is_high, zero, halo)
        return jnp.concatenate([low, inner, high], axis=axis)

    x_slab = swap(toward(volume, 2, high_x), 1)
    y_slab = swap(toward(volume, 1, high_y), 3)
    corner = swap(toward(toward(volume, 2, high_x), 1, high_y), 2)
    rows = place(volume, x_slab, 2, high_x)
    edge = place(y_slab, corner, 2, high_x)
    return place(rows, edge, 1, high_y)


def z_halo(volume, axis, radius):
    length = volume.shape[axis]
    nsp = lax.axis_size("space")
    first = lax.slice_in_dim(volume, 0, radius, axis=axis)
    last = lax.slice_in_dim(volume, length - radius, length, axis=axis)
    low = lax.ppermute(last, "space", [(i, i + ROW) for i in range(nsp - ROW)])
    high = lax.ppermute(first, "space", [(i + ROW, i) for i in range(nsp - ROW)])
    return jnp.concatenate([low, volume, high], axis=axis)


RS_BITS = (1, 4, 8, 2)


def bit_axis(present, m):
    order = [8, 4, 2, 1]
    return 1 + sum(1 for b in order if b in present and order.index(b) < order.index(m))


def view_reduce_scatter(full, nv):
    me = lax.axis_index("view")
    s0, s1, s2 = full.shape
    x = full.reshape(s0, 2, 2, 2, 2, s1 // nv, s2)
    present = {8, 4, 2, 1}
    for m in RS_BITS:
        ax = bit_axis(present, m)
        x0 = lax.index_in_dim(x, 0, axis=ax, keepdims=False)
        x1 = lax.index_in_dim(x, 1, axis=ax, keepdims=False)
        mine = (me & m) != 0
        keep = jnp.where(mine, x1, x0)
        send = jnp.where(mine, x0, x1)
        x = keep + lax.ppermute(send, "view", xor_pairs(nv, m))
        present.discard(m)
    return x


def view_all_gather(share, nv):
    me = lax.axis_index("view")
    x = share
    present = set()
    for m in reversed(RS_BITS):
        recv = lax.ppermute(x, "view", xor_pairs(nv, m))
        mine = (me & m) != 0
        lo = jnp.where(mine, recv, x)
        hi = jnp.where(mine, x, recv)
        ax = bit_axis(present | {m}, m)
        x = jnp.stack([lo, hi], axis=ax)
        present.add(m)
    s0 = x.shape[0]
    return x.reshape(s0, -1, x.shape[-1])


def shards(estimate, measured, kernel_x, kernel_y, kernel_z, neighbors, inside):
    side = estimate.shape[1]
    nsp = lax.axis_size("space")
    nv = lax.axis_size("view")
    me = lax.axis_index("space")
    table = gather_rows(
        jnp.concatenate([neighbors[0], inside.astype(jnp.int32)]), "space", nsp
    )
    nbr = table[:, :6]
    inside_all = table[:, 6]
    cx = (nbr[:, 0] >= 0).astype(jnp.int32)
    cy = (nbr[:, 2] >= 0).astype(jnp.int32)
    cz = jnp.zeros_like(cx)
    cur = nbr[:, 4]
    for _ in range(nsp // ROW - 1):
        cz = cz + (cur >= 0).astype(jnp.int32)
        cur = jnp.where(cur >= 0, nbr[jnp.maximum(cur, 0), 4], -1)
    ypos = jnp.where(cy == 0, cx, 3 - cx)
    place = cz * ROW + ypos
    ids = jnp.arange(nsp, dtype=jnp.int32)
    brick_at = jnp.zeros_like(place).at[place].set(ids)
    my_brick = brick_at[me]
    keep = inside_all[my_brick] > 0
    my_x = cx[my_brick]
    my_y = cy[my_brick]

    share = jnp.transpose(estimate[0].reshape(side, estimate.shape[2] // side, side), (2, 1, 0))
    share = route(share, place, my_brick, nsp)
    recorded = jnp.transpose(measured[0, 0].reshape(side, side, side), (2, 1, 0))
    chunk = side // 4
    recorded = jnp.concatenate(
        [
            route(recorded[c * chunk:(c + 1) * chunk], place, my_brick, nsp, columns_first=c % 2 == 1)
            for c in range(4)
        ],
        axis=0,
    )

    radius_x = (kernel_x.shape[1] - 1) // 2
    radius_y = (kernel_y.shape[1] - 1) // 2
    radius_z = (kernel_z.shape[1] - 1) // 2
    along_x = normalized(kernel_x[0])
    along_y = normalized(kernel_y[0])
    along_z = normalized(kernel_z[0])
    bands = {
        (axis, flipped): band_matrix(taps, side, flipped)
        for axis, taps in ((2, along_x), (1, along_y), (0, along_z))
        for flipped in (False, True)
    }
    bands = lax.optimization_barrier(bands)
    for sweep_no in range(ITERS):
        full = view_all_gather(share, nv)
        blurred = convolve(xy_halo(full, radius_x, radius_y, my_x == 1, my_y == 1), bands[2, False], 2)
        blurred = convolve(blurred, bands[1, False], 1)
        blurred = convolve(z_halo(blurred, 0, radius_z), bands[0, False], 0)
        quotient = recorded / blurred
        spread = convolve(z_halo(quotient, 0, radius_z), bands[0, True], 0)
        spread = convolve(xy_halo(spread, radius_x, radius_y, my_x == 1, my_y == 1), bands[1, True], 1)
        spread = convolve(spread, bands[2, True], 2)
        summed = view_reduce_scatter(spread, nv)
        share = share * jnp.where(keep, summed / (nv * measured.shape[0]), 1.0)
    share = route(share, brick_at, place[me], nsp)
    return jnp.transpose(share, (2, 1, 0)).reshape(1, side, estimate.shape[2])


def solution(mesh):
    placed = (
        P("space", None, "view"),
        P("view", "space", None, None),
        P("view", None),
        P("view", None),
        P("view", None),
        P("space", None),
        P("space"),
    )
    return jax.shard_map(
        shards, mesh=mesh, in_specs=placed, out_specs=P("space", None, "view"), check_vma=False
    )
```

```python
import jax
import jax.numpy as jnp
from jax import lax
from jax.sharding import PartitionSpec as P

ITERS = 2
ROW = 4


def normalized(kernel):
    return kernel / jnp.sum(kernel)


def xor_pairs(n, m):
    return [(i, i ^ m) for i in range(n)]


def gather_rows(row, axis, n):
    me = lax.axis_index(axis)
    buf = jnp.where(jnp.arange(n)[:, None] == me, row, jnp.zeros_like(row))
    for shift in (0, 2):
        step = [lax.ppermute(buf, axis, xor_pairs(n, t << shift)) for t in (1, 2, 3)]
        buf = buf + step[0] + step[1] + step[2]
    return buf


def route(x, dest, src_of_me, nsp, columns_first=False):
    me = lax.axis_index("space")
    rows = nsp // ROW
    if columns_first:
        n1, n2 = rows, ROW
        first, second = (lambda s: s // ROW), (lambda s: s % ROW)
        put = lambda s2, s1: s1 * ROW + s2
    else:
        n1, n2 = ROW, rows
        first, second = (lambda s: s % ROW), (lambda s: s // ROW)
        put = lambda s2, s1: s2 * ROW + s1
    my1, my2 = first(me), second(me)
    dest1 = first(dest[me])
    zero = jnp.zeros_like(x)
    received = []
    for k in range(n1):
        part = jnp.where((dest1 - my1) % n1 == k, x, zero)
        if k:
            pairs = [(put(q2, q1), put(q2, (q1 + k) % n1)) for q2 in range(n2) for q1 in range(n1)]
            part = lax.ppermute(part, "space", pairs)
        received.append((part, dest[put(my2, (my1 - k) % n1)]))
    result = zero
    for j in range(n2):
        target = put((my2 + j) % n2, my1)
        part = zero
        for data, d in received:
            part = jnp.where(d == target, data, part)
        if j:
            pairs = [(put(q2, q1), put((q2 + j) % n2, q1)) for q2 in range(n2) for q1 in range(n1)]
            part = lax.ppermute(part, "space", pairs)
        result = jnp.where((my2 - second(src_of_me)) % n2 == j, part, result)
    return result


def band_matrix(kernel, length, flipped):
    radius = (kernel.shape[0] - 1) // 2
    offset = jnp.arange(length + 2 * radius)[None, :] - jnp.arange(length)[:, None]
    band = jnp.zeros(offset.shape, jnp.float32)
    for position in range(2 * radius + 1):
        weight = kernel[2 * radius - position] if flipped else kernel[position]
        band = jnp.where(offset == position, weight, band)
    return band


def convolve(extended, band, axis):
    hi = lax.Precision.HIGHEST
    if axis == 0:
        return jnp.einsum("ot,tab->oab", band, extended, precision=hi)
    if axis == 1:
        return jnp.einsum("ot,atb->aob", band, extended, precision=hi)
    return jnp.einsum("abt,ot->abo", extended, band, precision=hi)


def pair_halo(volume, axis, radius, partner, is_high):
    length = volume.shape[axis]
    first = lax.slice_in_dim(volume, 0, radius, axis=axis)
    last = lax.slice_in_dim(volume, length - radius, length, axis=axis)
    send = jnp.where(is_high, first, last)
    nsp = lax.axis_size("space")
    recv = lax.ppermute(send, "space", [(i, i ^ partner) for i in range(nsp)])
    zero = jnp.zeros_like(recv)
    low = jnp.where(is_high, recv, zero)
    high = jnp.where(is_high, zero, recv)
    return jnp.concatenate([low, volume, high], axis=axis)


def xy_halo(volume, radius_i, radius_j, high_x, high_y):
    nsp = lax.axis_size("space")
    length = volume.shape[1]

    def toward(slab, axis, is_high):
        radius = radius_i if axis == 2 else radius_j
        first = lax.slice_in_dim(slab, 0, radius, axis=axis)
        last = lax.slice_in_dim(slab, length - radius, length, axis=axis)
        return jnp.where(is_high, first, last)

    def swap(x, partner):
        return lax.ppermute(x, "space", [(i, i ^ partner) for i in range(nsp)])

    def place(inner, halo, axis, is_high):
        zero = jnp.zeros_like(halo)
        low = jnp.where(is_high, halo, zero)
        high = jnp.where(is_high, zero, halo)
        return jnp.concatenate([low, inner, high], axis=axis)

    x_slab = swap(toward(volume, 2, high_x), 1)
    y_slab = swap(toward(volume, 1, high_y), 3)
    corner = swap(toward(toward(volume, 2, high_x), 1, high_y), 2)
    rows = place(volume, x_slab, 2, high_x)
    edge = place(y_slab, corner, 2, high_x)
    return place(rows, edge, 1, high_y)


def z_halo(volume, axis, radius):
    length = volume.shape[axis]
    nsp = lax.axis_size("space")
    first = lax.slice_in_dim(volume, 0, radius, axis=axis)
    last = lax.slice_in_dim(volume, length - radius, length, axis=axis)
    low = lax.ppermute(last, "space", [(i, i + ROW) for i in range(nsp - ROW)])
    high = lax.ppermute(first, "space", [(i + ROW, i) for i in range(nsp - ROW)])
    return jnp.concatenate([low, volume, high], axis=axis)


RS_BITS = (1, 4, 8, 2)


def bit_axis(present, m):
    order = [8, 4, 2, 1]
    return 1 + sum(1 for b in order if b in present and order.index(b) < order.index(m))


def view_reduce_scatter(full, nv):
    me = lax.axis_index("view")
    s0, s1, s2 = full.shape
    x = full.reshape(s0, 2, 2, 2, 2, s1 // nv, s2)
    present = {8, 4, 2, 1}
    for m in RS_BITS:
        ax = bit_axis(present, m)
        x0 = lax.index_in_dim(x, 0, axis=ax, keepdims=False)
        x1 = lax.index_in_dim(x, 1, axis=ax, keepdims=False)
        mine = (me & m) != 0
        keep = jnp.where(mine, x1, x0)
        send = jnp.where(mine, x0, x1)
        x = keep + lax.ppermute(send, "view", xor_pairs(nv, m))
        present.discard(m)
    return x


def view_all_gather(share, nv):
    me = lax.axis_index("view")
    x = share
    present = set()
    for m in reversed(RS_BITS):
        recv = lax.ppermute(x, "view", xor_pairs(nv, m))
        mine = (me & m) != 0
        lo = jnp.where(mine, recv, x)
        hi = jnp.where(mine, x, recv)
        ax = bit_axis(present | {m}, m)
        x = jnp.stack([lo, hi], axis=ax)
        present.add(m)
    s0 = x.shape[0]
    return x.reshape(s0, -1, x.shape[-1])


def shards(estimate, measured, kernel_x, kernel_y, kernel_z, neighbors, inside):
    side = estimate.shape[1]
    nsp = lax.axis_size("space")
    nv = lax.axis_size("view")
    me = lax.axis_index("space")
    table = gather_rows(
        jnp.concatenate([neighbors[0], inside.astype(jnp.int32)]), "space", nsp
    )
    nbr = table[:, :6]
    inside_all = table[:, 6]
    cx = (nbr[:, 0] >= 0).astype(jnp.int32)
    cy = (nbr[:, 2] >= 0).astype(jnp.int32)
    cz = jnp.zeros_like(cx)
    cur = nbr[:, 4]
    for _ in range(nsp // ROW - 1):
        cz = cz + (cur >= 0).astype(jnp.int32)
        cur = jnp.where(cur >= 0, nbr[jnp.maximum(cur, 0), 4], -1)
    ypos = jnp.where(cy == 0, cx, 3 - cx)
    place = cz * ROW + ypos
    ids = jnp.arange(nsp, dtype=jnp.int32)
    brick_at = jnp.zeros_like(place).at[place].set(ids)
    my_brick = brick_at[me]
    keep = inside_all[my_brick] > 0
    my_x = cx[my_brick]
    my_y = cy[my_brick]

    share = jnp.transpose(estimate[0].reshape(side, estimate.shape[2] // side, side), (2, 1, 0))
    share = route(share, place, my_brick, nsp)
    recorded = jnp.transpose(measured[0, 0].reshape(side, side, side), (2, 1, 0))
    chunk = side // 8
    recorded = jnp.concatenate(
        [
            route(recorded[c * chunk:(c + 1) * chunk], place, my_brick, nsp, columns_first=c % 2 == 1)
            for c in range(8)
        ],
        axis=0,
    )

    radius_x = (kernel_x.shape[1] - 1) // 2
    radius_y = (kernel_y.shape[1] - 1) // 2
    radius_z = (kernel_z.shape[1] - 1) // 2
    along_x = normalized(kernel_x[0])
    along_y = normalized(kernel_y[0])
    along_z = normalized(kernel_z[0])
    bands = {
        (axis, flipped): band_matrix(taps, side, flipped)
        for axis, taps in ((2, along_x), (1, along_y), (0, along_z))
        for flipped in (False, True)
    }
    bands = lax.optimization_barrier(bands)
    for sweep_no in range(ITERS):
        full = view_all_gather(share, nv)
        blurred = convolve(xy_halo(full, radius_x, radius_y, my_x == 1, my_y == 1), bands[2, False], 2)
        blurred = convolve(blurred, bands[1, False], 1)
        blurred = convolve(z_halo(blurred, 0, radius_z), bands[0, False], 0)
        quotient = recorded / blurred
        spread = convolve(z_halo(quotient, 0, radius_z), bands[0, True], 0)
        spread = convolve(xy_halo(spread, radius_x, radius_y, my_x == 1, my_y == 1), bands[1, True], 1)
        spread = convolve(spread, bands[2, True], 2)
        summed = view_reduce_scatter(spread, nv)
        share = share * jnp.where(keep, summed / (nv * measured.shape[0]), 1.0)
    share = route(share, brick_at, place[me], nsp)
    return jnp.transpose(share, (2, 1, 0)).reshape(1, side, estimate.shape[2])


def solution(mesh):
    placed = (
        P("space", None, "view"),
        P("view", "space", None, None),
        P("view", None),
        P("view", None),
        P("view", None),
        P("space", None),
        P("space"),
    )
    return jax.shard_map(
        shards, mesh=mesh, in_specs=placed, out_specs=P("space", None, "view"), check_vma=False
    )
```

```python
import jax
import jax.numpy as jnp
from jax import lax
from jax.sharding import PartitionSpec as P

ITERS = 2
ROW = 4


def normalized(kernel):
    return kernel / jnp.sum(kernel)


def xor_pairs(n, m):
    return [(i, i ^ m) for i in range(n)]


def gather_rows(row, axis, n):
    me = lax.axis_index(axis)
    buf = jnp.where(jnp.arange(n)[:, None] == me, row, jnp.zeros_like(row))
    for shift in (0, 2):
        step = [lax.ppermute(buf, axis, xor_pairs(n, t << shift)) for t in (1, 2, 3)]
        buf = buf + step[0] + step[1] + step[2]
    return buf


def route(x, dest, src_of_me, nsp, columns_first=False):
    me = lax.axis_index("space")
    rows = nsp // ROW
    if columns_first:
        n1, n2 = rows, ROW
        first, second = (lambda s: s // ROW), (lambda s: s % ROW)
        put = lambda s2, s1: s1 * ROW + s2
    else:
        n1, n2 = ROW, rows
        first, second = (lambda s: s % ROW), (lambda s: s // ROW)
        put = lambda s2, s1: s2 * ROW + s1
    my1, my2 = first(me), second(me)
    zero = jnp.zeros_like(x)
    received = []
    for k in range(n1):
        part = x
        if k:
            pairs = [(put(q2, q1), put(q2, (q1 + k) % n1)) for q2 in range(n2) for q1 in range(n1)]
            part = lax.ppermute(part, "space", pairs)
        received.append((part, dest[put(my2, (my1 - k) % n1)]))
    result = zero
    for j in range(n2):
        target = put((my2 + j) % n2, my1)
        part = zero
        for data, d in received:
            part = jnp.where(d == target, data, part)
        if j:
            pairs = [(put(q2, q1), put((q2 + j) % n2, q1)) for q2 in range(n2) for q1 in range(n1)]
            part = lax.ppermute(part, "space", pairs)
        result = jnp.where((my2 - second(src_of_me)) % n2 == j, part, result)
    return result


def band_matrix(kernel, length, flipped):
    radius = (kernel.shape[0] - 1) // 2
    offset = jnp.arange(length + 2 * radius)[None, :] - jnp.arange(length)[:, None]
    band = jnp.zeros(offset.shape, jnp.float32)
    for position in range(2 * radius + 1):
        weight = kernel[2 * radius - position] if flipped else kernel[position]
        band = jnp.where(offset == position, weight, band)
    return band


def convolve(extended, band, axis):
    hi = lax.Precision.HIGHEST
    if axis == 0:
        return jnp.einsum("ot,tab->oab", band, extended, precision=hi)
    if axis == 1:
        return jnp.einsum("ot,atb->aob", band, extended, precision=hi)
    return jnp.einsum("abt,ot->abo", extended, band, precision=hi)


def pair_halo(volume, axis, radius, partner, is_high):
    length = volume.shape[axis]
    first = lax.slice_in_dim(volume, 0, radius, axis=axis)
    last = lax.slice_in_dim(volume, length - radius, length, axis=axis)
    send = jnp.where(is_high, first, last)
    nsp = lax.axis_size("space")
    recv = lax.ppermute(send, "space", [(i, i ^ partner) for i in range(nsp)])
    zero = jnp.zeros_like(recv)
    low = jnp.where(is_high, recv, zero)
    high = jnp.where(is_high, zero, recv)
    return jnp.concatenate([low, volume, high], axis=axis)


def xy_halo(volume, radius_i, radius_j, high_x, high_y):
    nsp = lax.axis_size("space")
    length = volume.shape[1]

    def toward(slab, axis, is_high):
        radius = radius_i if axis == 2 else radius_j
        first = lax.slice_in_dim(slab, 0, radius, axis=axis)
        last = lax.slice_in_dim(slab, length - radius, length, axis=axis)
        return jnp.where(is_high, first, last)

    def swap(x, partner):
        return lax.ppermute(x, "space", [(i, i ^ partner) for i in range(nsp)])

    def place(inner, halo, axis, is_high):
        zero = jnp.zeros_like(halo)
        low = jnp.where(is_high, halo, zero)
        high = jnp.where(is_high, zero, halo)
        return jnp.concatenate([low, inner, high], axis=axis)

    x_slab = swap(toward(volume, 2, high_x), 1)
    y_slab = swap(toward(volume, 1, high_y), 3)
    corner = swap(toward(toward(volume, 2, high_x), 1, high_y), 2)
    rows = place(volume, x_slab, 2, high_x)
    edge = place(y_slab, corner, 2, high_x)
    return place(rows, edge, 1, high_y)


def z_halo(volume, axis, radius):
    length = volume.shape[axis]
    nsp = lax.axis_size("space")
    first = lax.slice_in_dim(volume, 0, radius, axis=axis)
    last = lax.slice_in_dim(volume, length - radius, length, axis=axis)
    low = lax.ppermute(last, "space", [(i, i + ROW) for i in range(nsp - ROW)])
    high = lax.ppermute(first, "space", [(i + ROW, i) for i in range(nsp - ROW)])
    return jnp.concatenate([low, volume, high], axis=axis)


RS_BITS = (1, 4, 8, 2)


def bit_axis(present, m):
    order = [8, 4, 2, 1]
    return 1 + sum(1 for b in order if b in present and order.index(b) < order.index(m))


def view_reduce_scatter(full, nv):
    me = lax.axis_index("view")
    s0, s1, s2 = full.shape
    x = full.reshape(s0, 2, 2, 2, 2, s1 // nv, s2)
    present = {8, 4, 2, 1}
    for m in RS_BITS:
        ax = bit_axis(present, m)
        x0 = lax.index_in_dim(x, 0, axis=ax, keepdims=False)
        x1 = lax.index_in_dim(x, 1, axis=ax, keepdims=False)
        mine = (me & m) != 0
        keep = jnp.where(mine, x1, x0)
        send = jnp.where(mine, x0, x1)
        x = keep + lax.ppermute(send, "view", xor_pairs(nv, m))
        present.discard(m)
    return x


def view_all_gather(share, nv):
    me = lax.axis_index("view")
    x = share
    present = set()
    for m in reversed(RS_BITS):
        recv = lax.ppermute(x, "view", xor_pairs(nv, m))
        mine = (me & m) != 0
        lo = jnp.where(mine, recv, x)
        hi = jnp.where(mine, x, recv)
        ax = bit_axis(present | {m}, m)
        x = jnp.stack([lo, hi], axis=ax)
        present.add(m)
    s0 = x.shape[0]
    return x.reshape(s0, -1, x.shape[-1])


def shards(estimate, measured, kernel_x, kernel_y, kernel_z, neighbors, inside):
    side = estimate.shape[1]
    nsp = lax.axis_size("space")
    nv = lax.axis_size("view")
    me = lax.axis_index("space")
    table = gather_rows(
        jnp.concatenate([neighbors[0], inside.astype(jnp.int32)]), "space", nsp
    )
    nbr = table[:, :6]
    inside_all = table[:, 6]
    cx = (nbr[:, 0] >= 0).astype(jnp.int32)
    cy = (nbr[:, 2] >= 0).astype(jnp.int32)
    cz = jnp.zeros_like(cx)
    cur = nbr[:, 4]
    for _ in range(nsp // ROW - 1):
        cz = cz + (cur >= 0).astype(jnp.int32)
        cur = jnp.where(cur >= 0, nbr[jnp.maximum(cur, 0), 4], -1)
    ypos = jnp.where(cy == 0, cx, 3 - cx)
    place = cz * ROW + ypos
    ids = jnp.arange(nsp, dtype=jnp.int32)
    brick_at = jnp.zeros_like(place).at[place].set(ids)
    my_brick = brick_at[me]
    keep = inside_all[my_brick] > 0
    my_x = cx[my_brick]
    my_y = cy[my_brick]

    share = jnp.transpose(estimate[0].reshape(side, estimate.shape[2] // side, side), (2, 1, 0))
    share = route(share, place, my_brick, nsp)
    recorded = jnp.transpose(measured[0, 0].reshape(side, side, side), (2, 1, 0))
    chunk = side // 4
    recorded = jnp.concatenate(
        [
            route(recorded[c * chunk:(c + 1) * chunk], place, my_brick, nsp, columns_first=c % 2 == 1)
            for c in range(4)
        ],
        axis=0,
    )

    radius_x = (kernel_x.shape[1] - 1) // 2
    radius_y = (kernel_y.shape[1] - 1) // 2
    radius_z = (kernel_z.shape[1] - 1) // 2
    along_x = normalized(kernel_x[0])
    along_y = normalized(kernel_y[0])
    along_z = normalized(kernel_z[0])
    bands = {
        (axis, flipped): band_matrix(taps, side, flipped)
        for axis, taps in ((2, along_x), (1, along_y), (0, along_z))
        for flipped in (False, True)
    }
    bands = lax.optimization_barrier(bands)
    for sweep_no in range(ITERS):
        full = view_all_gather(share, nv)
        blurred = convolve(xy_halo(full, radius_x, radius_y, my_x == 1, my_y == 1), bands[2, False], 2)
        blurred = convolve(blurred, bands[1, False], 1)
        blurred = convolve(z_halo(blurred, 0, radius_z), bands[0, False], 0)
        quotient = recorded / blurred
        spread = convolve(z_halo(quotient, 0, radius_z), bands[0, True], 0)
        spread = convolve(xy_halo(spread, radius_x, radius_y, my_x == 1, my_y == 1), bands[1, True], 1)
        spread = convolve(spread, bands[2, True], 2)
        summed = view_reduce_scatter(spread, nv)
        share = share * jnp.where(keep, summed / (nv * measured.shape[0]), 1.0)
    share = route(share, brick_at, place[me], nsp)
    return jnp.transpose(share, (2, 1, 0)).reshape(1, side, estimate.shape[2])


def solution(mesh):
    placed = (
        P("space", None, "view"),
        P("view", "space", None, None),
        P("view", None),
        P("view", None),
        P("view", None),
        P("space", None),
        P("space"),
    )
    return jax.shard_map(
        shards, mesh=mesh, in_specs=placed, out_specs=P("space", None, "view"), check_vma=False
    )
```

```python
import jax
import jax.numpy as jnp
from jax import lax
from jax.sharding import PartitionSpec as P

ITERS = 2
ROW = 4


def normalized(kernel):
    return kernel / jnp.sum(kernel)


def xor_pairs(n, m):
    return [(i, i ^ m) for i in range(n)]


def gather_rows(row, axis, n):
    me = lax.axis_index(axis)
    buf = jnp.where(jnp.arange(n)[:, None] == me, row, jnp.zeros_like(row))
    for shift in (0, 2):
        step = [lax.ppermute(buf, axis, xor_pairs(n, t << shift)) for t in (1, 2, 3)]
        buf = buf + step[0] + step[1] + step[2]
    return buf


def route(x, dest, src_of_me, nsp, columns_first=False):
    me = lax.axis_index("space")
    rows = nsp // ROW
    if columns_first:
        n1, n2 = rows, ROW
        first, second = (lambda s: s // ROW), (lambda s: s % ROW)
        put = lambda s2, s1: s1 * ROW + s2
    else:
        n1, n2 = ROW, rows
        first, second = (lambda s: s % ROW), (lambda s: s // ROW)
        put = lambda s2, s1: s2 * ROW + s1
    my1, my2 = first(me), second(me)
    dest1 = first(dest[me])
    zero = jnp.zeros_like(x)
    received = []
    for k in range(n1):
        part = jnp.where((dest1 - my1) % n1 == k, x, zero)
        if k:
            pairs = [(put(q2, q1), put(q2, (q1 + k) % n1)) for q2 in range(n2) for q1 in range(n1)]
            part = lax.ppermute(part, "space", pairs)
        received.append((part, dest[put(my2, (my1 - k) % n1)]))
    result = zero
    for j in range(n2):
        target = put((my2 + j) % n2, my1)
        part = zero
        for data, d in received:
            part = jnp.where(d == target, data, part)
        if j:
            pairs = [(put(q2, q1), put((q2 + j) % n2, q1)) for q2 in range(n2) for q1 in range(n1)]
            part = lax.ppermute(part, "space", pairs)
        result = jnp.where((my2 - second(src_of_me)) % n2 == j, part, result)
    return result


def band_matrix(kernel, length, flipped):
    radius = (kernel.shape[0] - 1) // 2
    offset = jnp.arange(length + 2 * radius)[None, :] - jnp.arange(length)[:, None]
    band = jnp.zeros(offset.shape, jnp.float32)
    for position in range(2 * radius + 1):
        weight = kernel[2 * radius - position] if flipped else kernel[position]
        band = jnp.where(offset == position, weight, band)
    return band


def convolve(extended, band, axis):
    hi = lax.Precision.HIGHEST
    if axis == 0:
        return jnp.einsum("ot,tab->oab", band, extended, precision=hi)
    if axis == 1:
        return jnp.einsum("ot,atb->aob", band, extended, precision=hi)
    return jnp.einsum("abt,ot->abo", extended, band, precision=hi)


def pair_halo(volume, axis, radius, partner, is_high):
    length = volume.shape[axis]
    first = lax.slice_in_dim(volume, 0, radius, axis=axis)
    last = lax.slice_in_dim(volume, length - radius, length, axis=axis)
    send = jnp.where(is_high, first, last)
    nsp = lax.axis_size("space")
    recv = lax.ppermute(send, "space", [(i, i ^ partner) for i in range(nsp)])
    zero = jnp.zeros_like(recv)
    low = jnp.where(is_high, recv, zero)
    high = jnp.where(is_high, zero, recv)
    return jnp.concatenate([low, volume, high], axis=axis)


def xy_halo(volume, radius_i, radius_j, high_x, high_y):
    nsp = lax.axis_size("space")
    length = volume.shape[1]

    def toward(slab, axis, is_high):
        radius = radius_i if axis == 2 else radius_j
        first = lax.slice_in_dim(slab, 0, radius, axis=axis)
        last = lax.slice_in_dim(slab, length - radius, length, axis=axis)
        return jnp.where(is_high, first, last)

    def swap(x, partner):
        return lax.ppermute(x, "space", [(i, i ^ partner) for i in range(nsp)])

    def place(inner, halo, axis, is_high):
        zero = jnp.zeros_like(halo)
        low = jnp.where(is_high, halo, zero)
        high = jnp.where(is_high, zero, halo)
        return jnp.concatenate([low, inner, high], axis=axis)

    x_slab = swap(toward(volume, 2, high_x), 1)
    y_slab = swap(toward(volume, 1, high_y), 3)
    corner = swap(toward(toward(volume, 2, high_x), 1, high_y), 2)
    rows = place(volume, x_slab, 2, high_x)
    edge = place(y_slab, corner, 2, high_x)
    return place(rows, edge, 1, high_y)


def z_halo(volume, axis, radius):
    length = volume.shape[axis]
    nsp = lax.axis_size("space")
    first = lax.slice_in_dim(volume, 0, radius, axis=axis)
    last = lax.slice_in_dim(volume, length - radius, length, axis=axis)
    low = lax.ppermute(last, "space", [(i, i + ROW) for i in range(nsp - ROW)])
    high = lax.ppermute(first, "space", [(i + ROW, i) for i in range(nsp - ROW)])
    return jnp.concatenate([low, volume, high], axis=axis)


RS_BITS = (1, 4, 8, 2)


def bit_axis(present, m):
    order = [8, 4, 2, 1]
    return 1 + sum(1 for b in order if b in present and order.index(b) < order.index(m))


def view_reduce_scatter(full, nv):
    me = lax.axis_index("view")
    s0, s1, s2 = full.shape
    x = full.reshape(s0, 2, 2, 2, 2, s1 // nv, s2)
    present = {8, 4, 2, 1}
    for m in RS_BITS:
        ax = bit_axis(present, m)
        x0 = lax.index_in_dim(x, 0, axis=ax, keepdims=False)
        x1 = lax.index_in_dim(x, 1, axis=ax, keepdims=False)
        mine = (me & m) != 0
        keep = jnp.where(mine, x1, x0)
        send = jnp.where(mine, x0, x1)
        x = keep + lax.ppermute(send, "view", xor_pairs(nv, m))
        present.discard(m)
    return x


def view_all_gather(share, nv):
    me = lax.axis_index("view")
    x = share
    present = set()
    for m in reversed(RS_BITS):
        recv = lax.ppermute(x, "view", xor_pairs(nv, m))
        mine = (me & m) != 0
        lo = jnp.where(mine, recv, x)
        hi = jnp.where(mine, x, recv)
        ax = bit_axis(present | {m}, m)
        x = jnp.stack([lo, hi], axis=ax)
        present.add(m)
    s0 = x.shape[0]
    return x.reshape(s0, -1, x.shape[-1])


def shards(estimate, measured, kernel_x, kernel_y, kernel_z, neighbors, inside):
    side = estimate.shape[1]
    nsp = lax.axis_size("space")
    nv = lax.axis_size("view")
    me = lax.axis_index("space")
    table = gather_rows(
        jnp.concatenate([neighbors[0], inside.astype(jnp.int32)]), "space", nsp
    )
    nbr = table[:, :6]
    inside_all = table[:, 6]
    cx = (nbr[:, 0] >= 0).astype(jnp.int32)
    cy = (nbr[:, 2] >= 0).astype(jnp.int32)
    cz = jnp.zeros_like(cx)
    cur = nbr[:, 4]
    for _ in range(nsp // ROW - 1):
        cz = cz + (cur >= 0).astype(jnp.int32)
        cur = jnp.where(cur >= 0, nbr[jnp.maximum(cur, 0), 4], -1)
    ypos = jnp.where(cy == 0, cx, 3 - cx)
    place = cz * ROW + ypos
    ids = jnp.arange(nsp, dtype=jnp.int32)
    brick_at = jnp.zeros_like(place).at[place].set(ids)
    my_brick = brick_at[me]
    keep = inside_all[my_brick] > 0
    my_x = cx[my_brick]
    my_y = cy[my_brick]

    share = jnp.transpose(estimate[0].reshape(side, estimate.shape[2] // side, side), (2, 1, 0))
    recorded = jnp.transpose(measured[0, 0].reshape(side, side, side), (2, 1, 0))
    chunk = side // 4
    share_planes = share.size // (side * side)
    parts = [
        jnp.concatenate([share.reshape(share_planes, side, side), recorded[:chunk]], axis=0)
    ] + [recorded[c * chunk:(c + 1) * chunk] for c in range(1, 4)]
    parts = [route(p, place, my_brick, nsp, columns_first=c % 2 == 1) for c, p in enumerate(parts)]
    share = parts[0][:share_planes].reshape(share.shape)
    recorded = jnp.concatenate([parts[0][share_planes:]] + parts[1:], axis=0)

    radius_x = (kernel_x.shape[1] - 1) // 2
    radius_y = (kernel_y.shape[1] - 1) // 2
    radius_z = (kernel_z.shape[1] - 1) // 2
    along_x = normalized(kernel_x[0])
    along_y = normalized(kernel_y[0])
    along_z = normalized(kernel_z[0])
    bands = {
        (axis, flipped): band_matrix(taps, side, flipped)
        for axis, taps in ((2, along_x), (1, along_y), (0, along_z))
        for flipped in (False, True)
    }
    bands = lax.optimization_barrier(bands)
    for sweep_no in range(ITERS):
        full = view_all_gather(share, nv)
        blurred = convolve(xy_halo(full, radius_x, radius_y, my_x == 1, my_y == 1), bands[2, False], 2)
        blurred = convolve(blurred, bands[1, False], 1)
        blurred = convolve(z_halo(blurred, 0, radius_z), bands[0, False], 0)
        quotient = recorded / blurred
        spread = convolve(z_halo(quotient, 0, radius_z), bands[0, True], 0)
        spread = convolve(xy_halo(spread, radius_x, radius_y, my_x == 1, my_y == 1), bands[1, True], 1)
        spread = convolve(spread, bands[2, True], 2)
        summed = view_reduce_scatter(spread, nv)
        share = share * jnp.where(keep, summed / (nv * measured.shape[0]), 1.0)
    share = route(share, brick_at, place[me], nsp)
    return jnp.transpose(share, (2, 1, 0)).reshape(1, side, estimate.shape[2])


def solution(mesh):
    placed = (
        P("space", None, "view"),
        P("view", "space", None, None),
        P("view", None),
        P("view", None),
        P("view", None),
        P("space", None),
        P("space"),
    )
    return jax.shard_map(
        shards, mesh=mesh, in_specs=placed, out_specs=P("space", None, "view"), check_vma=False
    )
```
